256 devices in a mesh: seq: 64 (over y, z, core), txt: 4 (over x).
Axes of the slice: x: 4, y: 4, z: 8, core: 2. Of those that a mesh axis runs over, the one named last changes fastest.
Arguments:
- self_q: bfloat16 [24576, 1024], P('seq', 'txt'), may hold values from -8 to 8
- self_k: bfloat16 [24576, 1024], P('seq', 'txt'), may hold values from -8 to 8
- self_v: bfloat16 [24576, 1024], P('seq', 'txt'), may hold values from -6 to 6
- cross_q: bfloat16 [24576, 1024], P('seq', 'txt'), may hold values from -8 to 8
- text_k: bfloat16 [4096, 1024], P('txt'), may hold values from -8 to 8
- text_v: bfloat16 [4096, 1024], P('txt'), may hold values from -6 to 6
- lags: int32 [192], P('seq'), may hold values from 1 to 32, as said below
Outputs:
- self_out: bfloat16 [24576, 1024], P('seq', 'txt')
- cross_out: bfloat16 [24576, 1024], P('seq', 'txt')
The draws below stay inside these ranges and needn't reach their ends.
Inputs may be any that keep to these rules, and one draw needn't show every extreme that they name: lags never fall from one span to the next; the last span sees all 32 blocks.
All inputs are finite; a program needn't handle non-finite values.
Results may differ from the reference program's by a relative error of at most 0.014.
Values may be sent and summed in bfloat16 or wider, within the bound.
No kernel may reach another device: no remote copies, remote signals or barrier semaphores. Data moves between devices by JAX's collectives and lax.ppermute only.
A program may use at most 128 MiB of HBM per device.

```python
import math
import jax
import jax.numpy as jnp
from jax import lax

HEADS = 8
HSIZE = 128
SPAN = 128
TBLK = 128
FRAMES = 24576
TEXT = 4096
HD = 1024


def drawn_draw(key, rows, salt):
    width = HEADS * HSIZE
    base = jax.random.normal(jax.random.fold_in(key, salt), (rows, width), jnp.float32)
    return jnp.clip(base, -8.0, 8.0).astype(jnp.bfloat16)


def draw_self_q(key, part):
    return drawn_draw(key, FRAMES, 11)


def draw_self_k(key, part):
    return drawn_draw(key, FRAMES, 23)


def draw_cross_q(key, part):
    return drawn_draw(key, FRAMES, 37)


def draw_text_k(key, part):
    return drawn_draw(key, TEXT, 53)


def draw_lags(key, part):
    count = FRAMES // SPAN
    top = TEXT // TBLK
    steps = jax.random.randint(jax.random.fold_in(key, 71), (count,), 1, 5)
    running = jnp.cumsum(steps)
    return (1 + (top - 1) * running // running[-1]).astype(jnp.int32)


def levels(stream_key, shape, pieces, smallest, largest):
    gain, own = 1.0, jax.random.fold_in(stream_key, 6)
    for axis_at, parts in pieces:
        heights = jnp.exp(jax.random.uniform(jax.random.fold_in(own, axis_at), (parts,), jnp.float32, smallest / len(pieces), largest / len(pieces)))
        gain = gain * jnp.repeat(heights, shape[axis_at] // parts).reshape([-1 if axis == axis_at else 1 for axis in range(len(shape))])
    return gain


def gaussian(own_key, shape, spread, most, shards=(), kind=jnp.bfloat16):
    array = jax.random.normal(own_key, shape, jnp.float32) * spread
    if len(shards) > 0:
        array = levels(own_key, shape, shards, -0.22, 0.18) * array
    return jnp.clip(array, min=-most, max=most).astype(kind)


def setup_inputs(seed: int = 0) -> dict:
    seeds = jax.random.split(jax.random.key(seed), 8)
    return {
        "self_q": draw_self_q(jax.random.fold_in(seeds[7], 71), 0),
        "self_k": draw_self_k(jax.random.fold_in(seeds[7], 71), 0),
        "self_v": gaussian(seeds[2], (FRAMES, HD), 1.0, 6.0, ((0, 64), (1, 4))),
        "cross_q": draw_cross_q(jax.random.fold_in(seeds[7], 71), 0),
        "text_k": draw_text_k(jax.random.fold_in(seeds[7], 71), 0),
        "text_v": gaussian(seeds[5], (TEXT, HD), 1.0, 6.0, ((0, 4),)),
        "lags": draw_lags(jax.random.fold_in(seeds[7], 71), 0),
    }


def attend(query, keys, values, visible):
    factor = 1.0 / math.sqrt(HSIZE)
    scores = jnp.einsum('qhd,khd->hqk', query.astype(jnp.float32), keys, preferred_element_type=jnp.float32) * factor
    scores = jnp.where(visible[None], scores, -jnp.inf)
    peak = lax.optimization_barrier(jnp.max(scores, axis=2))
    probs = jnp.exp(scores - peak[:, :, None])
    totals = lax.optimization_barrier(jnp.sum(probs, axis=2))
    weights = lax.optimization_barrier(probs.astype(jnp.bfloat16)).astype(jnp.float32)
    mixed = jnp.einsum('hqk,khd->qhd', weights, values, preferred_element_type=jnp.float32)
    mixed = mixed / jnp.transpose(totals)[:, :, None]
    return mixed.reshape(mixed.shape[0], HEADS * HSIZE).astype(jnp.bfloat16)

def reference(self_q, self_k, self_v, cross_q, text_k, text_v, lags):
    block = 512 if FRAMES % 512 == 0 else FRAMES
    count = FRAMES // block
    keys = self_k.astype(jnp.float32).reshape(FRAMES, HEADS, HSIZE)
    values = self_v.astype(jnp.float32).reshape(FRAMES, HEADS, HSIZE)
    text_keys = text_k.astype(jnp.float32).reshape(TEXT, HEADS, HSIZE)
    text_values = text_v.astype(jnp.float32).reshape(TEXT, HEADS, HSIZE)
    limits = (jnp.repeat(lags, SPAN) * TBLK).astype(jnp.int32)
    frame_pos = jnp.arange(FRAMES, dtype=jnp.int32)
    text_pos = jnp.arange(TEXT, dtype=jnp.int32)

    def self_block(number):
        first = (number * block).astype(jnp.int32)
        rows = lax.dynamic_slice_in_dim(self_q, first, block, 0).reshape(block, HEADS, HSIZE)
        query_pos = first + jnp.arange(block, dtype=jnp.int32)
        visible = frame_pos[None, :] <= query_pos[:, None]
        return attend(rows, keys, values, visible)

    def cross_block(number):
        first = (number * block).astype(jnp.int32)
        rows = lax.dynamic_slice_in_dim(cross_q, first, block, 0).reshape(block, HEADS, HSIZE)
        bound = lax.dynamic_slice_in_dim(limits, first, block, 0)
        visible = text_pos[None, :] < bound[:, None]
        return attend(rows, text_keys, text_values, visible)
    numbers = jnp.arange(count, dtype=jnp.int32)
    self_out = lax.map(self_block, numbers).reshape(FRAMES, HEADS * HSIZE)
    cross_out = lax.map(cross_block, numbers).reshape(FRAMES, HEADS * HSIZE)
    return (self_out, cross_out)
```

```python
import functools
import math

import jax
import jax.numpy as jnp
import numpy as np
from jax import lax
from jax.experimental import pallas as pl
from jax.experimental.pallas import tpu as pltpu
from jax.sharding import Mesh
from jax.sharding import PartitionSpec as P

HSIZE = 128
SPAN = 128
TBLK = 128

NEG_FILL = -1e30
FACTOR = 1.0 / math.sqrt(HSIZE)


def online_step(q, k, v, mask, m_ref, l_ref, acc_ref):
    scores = (
        lax.dot_general(q, k, (((1,), (1,)), ((), ())), preferred_element_type=jnp.float32)
        * FACTOR
    )
    if mask is not None:
        scores = jnp.where(mask, scores, NEG_FILL)
    m_prev = m_ref[...]
    m_next = jnp.maximum(m_prev, jnp.max(scores, axis=1, keepdims=True))
    probs = jnp.exp(scores - m_next[:, 0:1])
    if mask is not None:
        probs = jnp.where(mask, probs, 0.0)
    alpha = jnp.exp(m_prev - m_next)
    l_ref[...] = alpha * l_ref[...] + jnp.sum(probs, axis=1, keepdims=True)
    mixed = jnp.dot(probs.astype(jnp.bfloat16), v, preferred_element_type=jnp.float32)
    acc_ref[...] = acc_ref[...] * alpha + mixed
    m_ref[...] = m_next


def self_kernel(info_ref, q_ref, k_ref, v_ref, o_ref, lse_ref, m_ref, l_ref, acc_ref):
    t = pl.program_id(0)
    kb = pl.program_id(1)
    nkb = pl.num_programs(1)
    qblk = info_ref[t]
    core = info_ref[2]
    last = (qblk - core + 2) // 2 - 1

    @pl.when(kb == 0)
    def _():
        m_ref[...] = jnp.full(m_ref.shape, NEG_FILL, jnp.float32)
        l_ref[...] = jnp.zeros(l_ref.shape, jnp.float32)
        acc_ref[...] = jnp.zeros(acc_ref.shape, jnp.float32)

    diag = 2 * kb + core == qblk

    @pl.when(jnp.logical_and(kb <= last, jnp.logical_not(diag)))
    def _():
        online_step(q_ref[...], k_ref[...], v_ref[...], None, m_ref, l_ref, acc_ref)

    @pl.when(jnp.logical_and(kb <= last, diag))
    def _():
        rows = q_ref.shape[0]
        cols = k_ref.shape[0]
        r = lax.broadcasted_iota(jnp.int32, (rows, cols), 0)
        j = lax.broadcasted_iota(jnp.int32, (rows, cols), 1)
        online_step(q_ref[...], k_ref[...], v_ref[...], j <= r, m_ref, l_ref, acc_ref)

    @pl.when(kb == nkb - 1)
    def _():
        l = l_ref[...]
        seen = l > 0.0
        o_ref[...] = acc_ref[...] / jnp.where(seen, l, 1.0)
        lse_ref[...] = jnp.where(seen, m_ref[...] + jnp.log(jnp.where(seen, l, 1.0)), NEG_FILL)


def self_partial(info, q2, keys, values):
    block = q2.shape[0] // 2
    nkb = keys.shape[0] // block

    def kv_map(t, kb, info_ref):
        last = (info_ref[t] - info_ref[2] + 2) // 2 - 1
        return (jnp.maximum(jnp.minimum(kb, last), 0), 0)

    grid_spec = pltpu.PrefetchScalarGridSpec(
        num_scalar_prefetch=1,
        grid=(2, nkb),
        in_specs=[
            pl.BlockSpec((block, HSIZE), lambda t, kb, info_ref: (t, 0)),
            pl.BlockSpec((block, HSIZE), kv_map),
            pl.BlockSpec((block, HSIZE), kv_map),
        ],
        out_specs=[
            pl.BlockSpec((block, HSIZE), lambda t, kb, info_ref: (t, 0)),
            pl.BlockSpec((block, HSIZE), lambda t, kb, info_ref: (t, 0)),
        ],
        scratch_shapes=[
            pltpu.VMEM((block, HSIZE), jnp.float32),
            pltpu.VMEM((block, HSIZE), jnp.float32),
            pltpu.VMEM((block, HSIZE), jnp.float32),
        ],
    )
    rows = q2.shape[0]
    flops = 2 * 2 * rows * keys.shape[0] * HSIZE // 2
    return pl.pallas_call(
        self_kernel,
        grid_spec=grid_spec,
        out_shape=[
            jax.ShapeDtypeStruct((rows, HSIZE), jnp.float32),
            jax.ShapeDtypeStruct((rows, HSIZE), jnp.float32),
        ],
        compiler_params=pltpu.CompilerParams(dimension_semantics=("arbitrary", "arbitrary")),
        cost_estimate=pl.CostEstimate(
            flops=flops,
            transcendentals=rows * keys.shape[0] // 2,
            bytes_accessed=keys.size * 2 + values.size * 2 + rows * HSIZE * 10,
        ),
    )(info, q2, keys, values)


def cross_kernel(info_ref, q_ref, k_ref, v_ref, o_ref, m_ref, l_ref, acc_ref):
    kb = pl.program_id(1)
    nkb = pl.num_programs(1)
    tk = k_ref.shape[0]
    rows = q_ref.shape[0]
    last = info_ref[3]

    @pl.when(kb == 0)
    def _():
        m_ref[...] = jnp.full(m_ref.shape, NEG_FILL, jnp.float32)
        l_ref[...] = jnp.zeros(l_ref.shape, jnp.float32)
        acc_ref[...] = jnp.zeros(acc_ref.shape, jnp.float32)

    @pl.when(kb <= last)
    def _():
        r = lax.broadcasted_iota(jnp.int32, (rows, tk), 0)
        j = lax.broadcasted_iota(jnp.int32, (rows, tk), 1) + kb * tk
        span = r // SPAN
        limit = jnp.where(span == 0, info_ref[0], jnp.where(span == 1, info_ref[1], info_ref[2]))
        online_step(q_ref[...], k_ref[...], v_ref[...], j < limit * TBLK, m_ref, l_ref, acc_ref)

    @pl.when(kb == nkb - 1)
    def _():
        o_ref[...] = (acc_ref[...] / l_ref[...]).astype(o_ref.dtype)


def cross_attention(info, query, keys, values):
    rows = query.shape[0]
    heads = query.shape[1] // HSIZE
    tk = 512
    nkb = keys.shape[0] // tk

    def kv_map(h, kb, info_ref):
        return (jnp.minimum(kb, info_ref[3]), h)

    grid_spec = pltpu.PrefetchScalarGridSpec(
        num_scalar_prefetch=1,
        grid=(heads, nkb),
        in_specs=[
            pl.BlockSpec((rows, HSIZE), lambda h, kb, info_ref: (0, h)),
            pl.BlockSpec((tk, HSIZE), kv_map),
            pl.BlockSpec((tk, HSIZE), kv_map),
        ],
        out_specs=pl.BlockSpec((rows, HSIZE), lambda h, kb, info_ref: (0, h)),
        scratch_shapes=[
            pltpu.VMEM((rows, HSIZE), jnp.float32),
            pltpu.VMEM((rows, HSIZE), jnp.float32),
            pltpu.VMEM((rows, HSIZE), jnp.float32),
        ],
    )
    return pl.pallas_call(
        cross_kernel,
        grid_spec=grid_spec,
        out_shape=jax.ShapeDtypeStruct(query.shape, jnp.bfloat16),
        compiler_params=pltpu.CompilerParams(dimension_semantics=("arbitrary", "arbitrary")),
        cost_estimate=pl.CostEstimate(
            flops=4 * rows * keys.shape[0] * query.shape[1],
            transcendentals=rows * keys.shape[0] * heads,
            bytes_accessed=keys.size * 2 + values.size * 2 + query.size * 4,
        ),
    )(info, query, keys, values)


def merge(o_a, lse_a, o_b, lse_b):
    top = jnp.maximum(lse_a, lse_b)
    w_a = jnp.exp(lse_a - top)
    w_b = jnp.exp(lse_b - top)
    return (o_a * w_a + o_b * w_b) / (w_a + w_b)


def per_device(self_q, self_k, self_v, cross_q, text_k, text_v, lags):
    rows = self_q.shape[0]
    heads = self_q.shape[1] // HSIZE
    chip = lax.axis_index("chip")
    core = lax.axis_index("core")
    swap = [(0, 1), (1, 0)]
    info = jnp.stack([2 * chip + core, 2 * chip + 1 - core, core]).astype(jnp.int32)

    whole_keys = lax.all_to_all(text_k, "txt", split_axis=1, concat_axis=0, tiled=True)
    whole_values = lax.all_to_all(text_v, "txt", split_axis=1, concat_axis=0, tiled=True)

    outs = []
    for h in range(heads):
        cols = slice(h * HSIZE, (h + 1) * HSIZE)
        q_h = self_q[:, cols]
        keys = lax.all_gather(self_k[:, cols], "chip", axis=0, tiled=True)
        values = lax.all_gather(self_v[:, cols], "chip", axis=0, tiled=True)
        q2 = jnp.concatenate([q_h, lax.ppermute(q_h, "core", swap)], axis=0)
        o_part, lse_part = self_partial(info, q2, keys, values)
        o_back = lax.ppermute(o_part[rows:], "core", swap)
        lse_back = lax.ppermute(lse_part[rows:], "core", swap)
        outs.append(merge(o_part[:rows], lse_part[:rows], o_back, lse_back).astype(jnp.bfloat16))
    self_out = jnp.concatenate(outs, axis=1)

    top = jnp.max(lags)
    cross_info = jnp.concatenate(
        [lags.astype(jnp.int32), ((top * TBLK - 1) // 512)[None].astype(jnp.int32)]
    )
    cross_out = cross_attention(cross_info, cross_q, whole_keys, whole_values)
    return (self_out, cross_out)


def solution(mesh):
    seq = mesh.shape["seq"]
    txt = mesh.shape["txt"]
    inner = Mesh(np.asarray(mesh.devices).reshape(seq // 2, 2, txt), ("chip", "core", "txt"))
    rows = P(("chip", "core"), "txt")
    return jax.shard_map(
        per_device,
        mesh=inner,
        in_specs=(rows, rows, rows, rows, P("txt", None), P("txt", None), P(("chip", "core"))),
        out_specs=(rows, rows),
        check_vma=False,
    )
```

```python
import functools
import math

import jax
import jax.numpy as jnp
import numpy as np
from jax import lax
from jax.experimental import pallas as pl
from jax.experimental.pallas import tpu as pltpu
from jax.sharding import Mesh
from jax.sharding import PartitionSpec as P

HSIZE = 128
SPAN = 128
TBLK = 128

NEG_FILL = -1e30
FACTOR = 1.0 / math.sqrt(HSIZE)


def online_step(q, k, v, mask, m_ref, l_ref, acc_ref):
    scores = (
        lax.dot_general(q, k, (((1,), (1,)), ((), ())), preferred_element_type=jnp.float32)
        * FACTOR
    )
    if mask is not None:
        scores = jnp.where(mask, scores, NEG_FILL)
    m_prev = m_ref[...]
    m_next = jnp.maximum(m_prev, jnp.max(scores, axis=1, keepdims=True))
    probs = jnp.exp(scores - m_next[:, 0:1])
    if mask is not None:
        probs = jnp.where(mask, probs, 0.0)
    alpha = jnp.exp(m_prev - m_next)
    l_ref[...] = alpha * l_ref[...] + jnp.sum(probs, axis=1, keepdims=True)
    mixed = jnp.dot(probs.astype(jnp.bfloat16), v, preferred_element_type=jnp.float32)
    acc_ref[...] = acc_ref[...] * alpha + mixed
    m_ref[...] = m_next


def self_kernel(info_ref, q_ref, k_ref, v_ref, o_ref, m_ref, l_ref, acc_ref):
    kb = pl.program_id(0)
    nkb = pl.num_programs(0)
    place = info_ref[0]
    last = info_ref[1]
    rows = q_ref.shape[0]
    tk = k_ref.shape[0]
    heads = q_ref.shape[1] // HSIZE

    @pl.when(kb == 0)
    def _():
        m_ref[...] = jnp.full(m_ref.shape, NEG_FILL, jnp.float32)
        l_ref[...] = jnp.zeros(l_ref.shape, jnp.float32)
        acc_ref[...] = jnp.zeros(acc_ref.shape, jnp.float32)

    def run(mask):
        for h in range(heads):
            cols = slice(h * HSIZE, (h + 1) * HSIZE)
            online_step(
                q_ref[:, cols], k_ref[:, cols], v_ref[:, cols], mask,
                m_ref.at[h], l_ref.at[h], acc_ref.at[h],
            )

    @pl.when(kb < last)
    def _():
        run(None)

    @pl.when(kb == last)
    def _():
        r = lax.broadcasted_iota(jnp.int32, (rows, tk), 0) + place * rows
        j = lax.broadcasted_iota(jnp.int32, (rows, tk), 1) + kb * tk
        run(j <= r)

    @pl.when(kb == nkb - 1)
    def _():
        for h in range(heads):
            o_ref[:, h * HSIZE:(h + 1) * HSIZE] = (acc_ref[h] / l_ref[h]).astype(o_ref.dtype)


def self_attention(info, query, kv, tk):
    rows, width = query.shape
    heads = width // HSIZE
    nkb = kv.shape[0] // tk

    def k_map(kb, info_ref):
        return (jnp.minimum(kb, info_ref[1]), 0)

    def v_map(kb, info_ref):
        return (jnp.minimum(kb, info_ref[1]), 1)

    grid_spec = pltpu.PrefetchScalarGridSpec(
        num_scalar_prefetch=1,
        grid=(nkb,),
        in_specs=[
            pl.BlockSpec((rows, width), lambda kb, info_ref: (0, 0)),
            pl.BlockSpec((tk, width), k_map),
            pl.BlockSpec((tk, width), v_map),
        ],
        out_specs=pl.BlockSpec((rows, width), lambda kb, info_ref: (0, 0)),
        scratch_shapes=[
            pltpu.VMEM((heads, rows, HSIZE), jnp.float32),
            pltpu.VMEM((heads, rows, HSIZE), jnp.float32),
            pltpu.VMEM((heads, rows, HSIZE), jnp.float32),
        ],
    )
    keys = kv.shape[0]
    return pl.pallas_call(
        self_kernel,
        grid_spec=grid_spec,
        out_shape=jax.ShapeDtypeStruct(query.shape, jnp.bfloat16),
        compiler_params=pltpu.CompilerParams(dimension_semantics=("arbitrary",)),
        cost_estimate=pl.CostEstimate(
            flops=2 * rows * keys * width,
            transcendentals=rows * keys * heads // 2,
            bytes_accessed=kv.size + query.size * 4,
        ),
    )(info, query, kv, kv)


def cross_kernel(info_ref, q_ref, k_ref, v_ref, o_ref, m_ref, l_ref, acc_ref):
    kb = pl.program_id(1)
    nkb = pl.num_programs(1)
    tk = k_ref.shape[0]
    rows = q_ref.shape[0]
    last = info_ref[3]

    @pl.when(kb == 0)
    def _():
        m_ref[...] = jnp.full(m_ref.shape, NEG_FILL, jnp.float32)
        l_ref[...] = jnp.zeros(l_ref.shape, jnp.float32)
        acc_ref[...] = jnp.zeros(acc_ref.shape, jnp.float32)

    @pl.when(kb <= last)
    def _():
        r = lax.broadcasted_iota(jnp.int32, (rows, tk), 0)
        j = lax.broadcasted_iota(jnp.int32, (rows, tk), 1) + kb * tk
        span = r // SPAN
        limit = jnp.where(span == 0, info_ref[0], jnp.where(span == 1, info_ref[1], info_ref[2]))
        online_step(q_ref[...], k_ref[...], v_ref[...], j < limit * TBLK, m_ref, l_ref, acc_ref)

    @pl.when(kb == nkb - 1)
    def _():
        o_ref[...] = (acc_ref[...] / l_ref[...]).astype(o_ref.dtype)


def cross_attention(info, query, keys, values):
    rows = query.shape[0]
    heads = query.shape[1] // HSIZE
    tk = 512
    nkb = keys.shape[0] // tk

    def kv_map(h, kb, info_ref):
        return (jnp.minimum(kb, info_ref[3]), h)

    grid_spec = pltpu.PrefetchScalarGridSpec(
        num_scalar_prefetch=1,
        grid=(heads, nkb),
        in_specs=[
            pl.BlockSpec((rows, HSIZE), lambda h, kb, info_ref: (0, h)),
            pl.BlockSpec((tk, HSIZE), kv_map),
            pl.BlockSpec((tk, HSIZE), kv_map),
        ],
        out_specs=pl.BlockSpec((rows, HSIZE), lambda h, kb, info_ref: (0, h)),
        scratch_shapes=[
            pltpu.VMEM((rows, HSIZE), jnp.float32),
            pltpu.VMEM((rows, HSIZE), jnp.float32),
            pltpu.VMEM((rows, HSIZE), jnp.float32),
        ],
    )
    return pl.pallas_call(
        cross_kernel,
        grid_spec=grid_spec,
        out_shape=jax.ShapeDtypeStruct(query.shape, jnp.bfloat16),
        compiler_params=pltpu.CompilerParams(dimension_semantics=("arbitrary", "arbitrary")),
        cost_estimate=pl.CostEstimate(
            flops=4 * rows * keys.shape[0] * query.shape[1],
            transcendentals=rows * keys.shape[0] * heads,
            bytes_accessed=keys.size * 2 + values.size * 2 + query.size * 4,
        ),
    )(info, query, keys, values)


def per_device(self_q, self_k, self_v, cross_q, text_k, text_v, lags):
    rows = self_q.shape[0]
    tk = 2 * rows
    place = lax.axis_index("seq")

    whole_keys = lax.all_to_all(text_k, "txt", split_axis=1, concat_axis=0, tiled=True)
    whole_values = lax.all_to_all(text_v, "txt", split_axis=1, concat_axis=0, tiled=True)

    kv = lax.all_gather(jnp.concatenate([self_k, self_v], axis=1), "seq", axis=0, tiled=True)
    info = jnp.stack([place, (place * rows + rows - 1) // tk]).astype(jnp.int32)
    self_out = self_attention(info, self_q, kv, tk)

    top = jnp.max(lags)
    cross_info = jnp.concatenate(
        [lags.astype(jnp.int32), ((top * TBLK - 1) // 512)[None].astype(jnp.int32)]
    )
    cross_out = cross_attention(cross_info, cross_q, whole_keys, whole_values)
    return (self_out, cross_out)


def solution(mesh):
    rows = P("seq", "txt")
    return jax.shard_map(
        per_device,
        mesh=mesh,
        in_specs=(rows, rows, rows, rows, P("txt", None), P("txt", None), P("seq")),
        out_specs=(rows, rows),
        check_vma=False,
    )
```

```python
import functools
import math

import jax
import jax.numpy as jnp
import numpy as np
from jax import lax
from jax.experimental import pallas as pl
from jax.experimental.pallas import tpu as pltpu
from jax.sharding import Mesh
from jax.sharding import PartitionSpec as P

HSIZE = 128
SPAN = 128
TBLK = 128

NEG_FILL = -1e30
FACTOR = 1.0 / math.sqrt(HSIZE)


def online_step(q, k, v, mask, m_ref, l_ref, acc_ref):
    scores = (
        lax.dot_general(q, k, (((1,), (1,)), ((), ())), preferred_element_type=jnp.float32)
        * FACTOR
    )
    if mask is not None:
        scores = jnp.where(mask, scores, NEG_FILL)
    m_prev = m_ref[...]
    m_next = jnp.maximum(m_prev, jnp.max(scores, axis=1, keepdims=True))
    probs = jnp.exp(scores - m_next[:, 0:1])
    if mask is not None:
        probs = jnp.where(mask, probs, 0.0)
    alpha = jnp.exp(m_prev - m_next)
    l_ref[...] = alpha * l_ref[...] + jnp.sum(probs, axis=1, keepdims=True)
    mixed = jnp.dot(probs.astype(jnp.bfloat16), v, preferred_element_type=jnp.float32)
    acc_ref[...] = acc_ref[...] * alpha + mixed
    m_ref[...] = m_next


def self_kernel(info_ref, q_ref, k_ref, v_ref, o_ref, lse_ref, m_ref, l_ref, acc_ref):
    kb = pl.program_id(0)
    nkb = pl.num_programs(0)
    qblk = info_ref[0]
    lo = info_ref[1]
    hi = info_ref[2]
    base = info_ref[3]
    top = info_ref[4]
    rows = q_ref.shape[0]
    tk = k_ref.shape[0]
    heads = q_ref.shape[1] // HSIZE
    blk = base + kb

    @pl.when(kb == 0)
    def _():
        m_ref[...] = jnp.full(m_ref.shape, NEG_FILL, jnp.float32)
        l_ref[...] = jnp.zeros(l_ref.shape, jnp.float32)
        acc_ref[...] = jnp.zeros(acc_ref.shape, jnp.float32)

    def run(mask):
        for h in range(heads):
            cols = slice(h * HSIZE, (h + 1) * HSIZE)
            online_step(
                q_ref[:, cols], k_ref[:, cols], v_ref[:, cols], mask,
                m_ref.at[h], l_ref.at[h], acc_ref.at[h],
            )

    live = blk <= top
    edge = jnp.logical_or(blk == base, blk == top)

    @pl.when(jnp.logical_and(live, jnp.logical_not(edge)))
    def _():
        run(None)

    @pl.when(jnp.logical_and(live, edge))
    def _():
        r = lax.broadcasted_iota(jnp.int32, (rows, tk), 0) + qblk * rows
        j = lax.broadcasted_iota(jnp.int32, (rows, tk), 1) + blk * tk
        inside = jnp.logical_and(j >= lo * rows, j < hi * rows)
        run(jnp.logical_and(j <= r, inside))

    @pl.when(kb == nkb - 1)
    def _():
        for h in range(heads):
            l = l_ref[h]
            seen = l > 0.0
            safe = jnp.where(seen, l, 1.0)
            o_ref[:, h * HSIZE:(h + 1) * HSIZE] = acc_ref[h] / safe
            lse_ref[h] = jnp.where(seen, m_ref[h] + jnp.log(safe), NEG_FILL)


def self_partial(qblk, lo, hi, query, kv, tk, steps):
    rows, width = query.shape
    heads = width // HSIZE
    per = tk // rows
    base = lo // per
    top = jnp.where(hi > lo, (hi - 1) // per, base - 1)
    info = jnp.stack([qblk, lo, hi, base, top, jnp.maximum(top, base)]).astype(jnp.int32)

    def k_map(kb, info_ref):
        return (jnp.minimum(info_ref[3] + kb, info_ref[5]), 0)

    def v_map(kb, info_ref):
        return (jnp.minimum(info_ref[3] + kb, info_ref[5]), 1)

    grid_spec = pltpu.PrefetchScalarGridSpec(
        num_scalar_prefetch=1,
        grid=(steps,),
        in_specs=[
            pl.BlockSpec((rows, width), lambda kb, info_ref: (0, 0)),
            pl.BlockSpec((tk, width), k_map),
            pl.BlockSpec((tk, width), v_map),
        ],
        out_specs=[
            pl.BlockSpec((rows, width), lambda kb, info_ref: (0, 0)),
            pl.BlockSpec((heads, rows, HSIZE), lambda kb, info_ref: (0, 0, 0)),
        ],
        scratch_shapes=[
            pltpu.VMEM((heads, rows, HSIZE), jnp.float32),
            pltpu.VMEM((heads, rows, HSIZE), jnp.float32),
            pltpu.VMEM((heads, rows, HSIZE), jnp.float32),
        ],
    )
    keys = steps * tk
    return pl.pallas_call(
        self_kernel,
        grid_spec=grid_spec,
        out_shape=[
            jax.ShapeDtypeStruct((rows, width), jnp.float32),
            jax.ShapeDtypeStruct((heads, rows, HSIZE), jnp.float32),
        ],
        compiler_params=pltpu.CompilerParams(dimension_semantics=("arbitrary",)),
        cost_estimate=pl.CostEstimate(
            flops=2 * rows * keys * width,
            transcendentals=rows * keys * heads,
            bytes_accessed=keys * width * 4 + query.size * 2 + rows * width * 8,
        ),
    )(info, query, kv, kv)


def spread(lse):
    heads, rows, _ = lse.shape
    return jnp.broadcast_to(jnp.transpose(lse, (1, 0, 2)), (rows, heads, HSIZE)).reshape(
        rows, heads * HSIZE
    )


def cross_kernel(info_ref, q_ref, k_ref, v_ref, o_ref, m_ref, l_ref, acc_ref):
    kb = pl.program_id(1)
    nkb = pl.num_programs(1)
    tk = k_ref.shape[0]
    rows = q_ref.shape[0]
    last = info_ref[3]

    @pl.when(kb == 0)
    def _():
        m_ref[...] = jnp.full(m_ref.shape, NEG_FILL, jnp.float32)
        l_ref[...] = jnp.zeros(l_ref.shape, jnp.float32)
        acc_ref[...] = jnp.zeros(acc_ref.shape, jnp.float32)

    @pl.when(kb <= last)
    def _():
        r = lax.broadcasted_iota(jnp.int32, (rows, tk), 0)
        j = lax.broadcasted_iota(jnp.int32, (rows, tk), 1) + kb * tk
        span = r // SPAN
        limit = jnp.where(span == 0, info_ref[0], jnp.where(span == 1, info_ref[1], info_ref[2]))
        online_step(q_ref[...], k_ref[...], v_ref[...], j < limit * TBLK, m_ref, l_ref, acc_ref)

    @pl.when(kb == nkb - 1)
    def _():
        o_ref[...] = (acc_ref[...] / l_ref[...]).astype(o_ref.dtype)


def cross_attention(info, query, keys, values):
    rows = query.shape[0]
    heads = query.shape[1] // HSIZE
    tk = 512
    nkb = keys.shape[0] // tk

    def kv_map(h, kb, info_ref):
        return (jnp.minimum(kb, info_ref[3]), h)

    grid_spec = pltpu.PrefetchScalarGridSpec(
        num_scalar_prefetch=1,
        grid=(heads, nkb),
        in_specs=[
            pl.BlockSpec((rows, HSIZE), lambda h, kb, info_ref: (0, h)),
            pl.BlockSpec((tk, HSIZE), kv_map),
            pl.BlockSpec((tk, HSIZE), kv_map),
        ],
        out_specs=pl.BlockSpec((rows, HSIZE), lambda h, kb, info_ref: (0, h)),
        scratch_shapes=[
            pltpu.VMEM((rows, HSIZE), jnp.float32),
            pltpu.VMEM((rows, HSIZE), jnp.float32),
            pltpu.VMEM((rows, HSIZE), jnp.float32),
        ],
    )
    return pl.pallas_call(
        cross_kernel,
        grid_spec=grid_spec,
        out_shape=jax.ShapeDtypeStruct(query.shape, jnp.bfloat16),
        compiler_params=pltpu.CompilerParams(dimension_semantics=("arbitrary", "arbitrary")),
        cost_estimate=pl.CostEstimate(
            flops=4 * rows * keys.shape[0] * query.shape[1],
            transcendentals=rows * keys.shape[0] * heads,
            bytes_accessed=keys.size * 2 + values.size * 2 + query.size * 4,
        ),
    )(info, query, keys, values)


def per_device(self_q, self_k, self_v, cross_q, text_k, text_v, lags):
    rows = self_q.shape[0]
    tk = 2 * rows
    place = lax.axis_index("seq")

    whole_keys = lax.all_to_all(text_k, "txt", split_axis=1, concat_axis=0, tiled=True)
    whole_values = lax.all_to_all(text_v, "txt", split_axis=1, concat_axis=0, tiled=True)

    kv = lax.all_gather(jnp.concatenate([self_k, self_v], axis=1), "seq", axis=0, tiled=True)
    blocks = kv.shape[0] // rows
    half = blocks // 2
    pairs = [(i, blocks - 1 - i) for i in range(blocks)]
    partner = blocks - 1 - place
    heavy = place >= half
    other_q = lax.ppermute(self_q, "seq", pairs)

    b_hi = jnp.where(heavy, 0, half - 1 - place)
    o_b, lse_b = self_partial(partner, 0, b_hi, other_q, kv, tk, half // 2)
    o_back = lax.ppermute(o_b, "seq", pairs)
    lse_back = lax.ppermute(lse_b[:, :, :1], "seq", pairs)

    a_lo = jnp.where(heavy, place - half, 0)
    o_a, lse_a = self_partial(place, a_lo, place + 1, self_q, kv, tk, (half + 1) // 2 + 1)
    la = spread(lse_a[:, :, :1])
    lb = spread(lse_back)
    peak = jnp.maximum(la, lb)
    w_a = jnp.exp(la - peak)
    w_b = jnp.exp(lb - peak)
    self_out = ((o_a * w_a + o_back * w_b) / (w_a + w_b)).astype(jnp.bfloat16)

    top = jnp.max(lags)
    cross_info = jnp.concatenate(
        [lags.astype(jnp.int32), ((top * TBLK - 1) // 512)[None].astype(jnp.int32)]
    )
    cross_out = cross_attention(cross_info, cross_q, whole_keys, whole_values)
    return (self_out, cross_out)


def solution(mesh):
    rows = P("seq", "txt")
    return jax.shard_map(
        per_device,
        mesh=mesh,
        in_specs=(rows, rows, rows, rows, P("txt", None), P("txt", None), P("seq")),
        out_specs=(rows, rows),
        check_vma=False,
    )
```

```python
import functools
import math

import jax
import jax.numpy as jnp
import numpy as np
from jax import lax
from jax.experimental import pallas as pl
from jax.experimental.pallas import tpu as pltpu
from jax.sharding import Mesh
from jax.sharding import PartitionSpec as P

HSIZE = 128
SPAN = 128
TBLK = 128

NEG_FILL = -1e30
FACTOR = 1.0 / math.sqrt(HSIZE)
SCALE2 = FACTOR * 1.4426950408889634


def online_step(q, k, v, mask, m_ref, l_ref, acc_ref):
    scores = (
        lax.dot_general(q, k, (((1,), (1,)), ((), ())), preferred_element_type=jnp.float32)
        * SCALE2
    )
    if mask is not None:
        scores = jnp.where(mask, scores, NEG_FILL)
    m_prev = m_ref[...]
    m_next = jnp.maximum(m_prev, jnp.max(scores, axis=1, keepdims=True))
    probs = jnp.exp2(scores - m_next[:, 0:1])
    if mask is not None:
        probs = jnp.where(mask, probs, 0.0)
    alpha = jnp.exp2(m_prev - m_next)
    extended = jnp.concatenate([v, jnp.ones_like(v)], axis=1)
    mixed = jnp.dot(probs.astype(jnp.bfloat16), extended, preferred_element_type=jnp.float32)
    l_ref[...] = alpha * l_ref[...] + mixed[:, HSIZE:]
    acc_ref[...] = acc_ref[...] * alpha + mixed[:, :HSIZE]
    m_ref[...] = m_next


def self_kernel(info_ref, q_ref, k_ref, v_ref, o_ref, lse_ref, m_ref, l_ref, acc_ref):
    kb = pl.program_id(0)
    nkb = pl.num_programs(0)
    qblk = info_ref[0]
    lo = info_ref[1]
    hi = info_ref[2]
    base = info_ref[3]
    top = info_ref[4]
    rows = q_ref.shape[0]
    tk = k_ref.shape[0]
    heads = q_ref.shape[1] // HSIZE
    blk = base + kb

    @pl.when(kb == 0)
    def _():
        m_ref[...] = jnp.full(m_ref.shape, NEG_FILL, jnp.float32)
        l_ref[...] = jnp.zeros(l_ref.shape, jnp.float32)
        acc_ref[...] = jnp.zeros(acc_ref.shape, jnp.float32)

    def run(mask):
        for h in range(heads):
            cols = slice(h * HSIZE, (h + 1) * HSIZE)
            online_step(
                q_ref[:, cols], k_ref[:, cols], v_ref[:, cols], mask,
                m_ref.at[h], l_ref.at[h], acc_ref.at[h],
            )

    live = blk <= top
    edge = jnp.logical_or(blk == base, blk == top)

    @pl.when(jnp.logical_and(live, jnp.logical_not(edge)))
    def _():
        run(None)

    @pl.when(jnp.logical_and(live, edge))
    def _():
        r = lax.broadcasted_iota(jnp.int32, (rows, tk), 0) + qblk * rows
        j = lax.broadcasted_iota(jnp.int32, (rows, tk), 1) + blk * tk
        inside = jnp.logical_and(j >= lo * rows, j < hi * rows)
        run(jnp.logical_and(j <= r, inside))

    @pl.when(kb == nkb - 1)
    def _():
        for h in range(heads):
            l = l_ref[h]
            seen = l > 0.0
            safe = jnp.where(seen, l, 1.0)
            o_ref[:, h * HSIZE:(h + 1) * HSIZE] = acc_ref[h] / safe
            lse_ref[h] = jnp.where(seen, m_ref[h] + jnp.log2(safe), NEG_FILL)


def self_partial(qblk, lo, hi, query, kv, tk, steps):
    rows, width = query.shape
    heads = width // HSIZE
    per = tk // rows
    base = lo // per
    top = jnp.where(hi > lo, (hi - 1) // per, base - 1)
    info = jnp.stack([qblk, lo, hi, base, top, jnp.maximum(top, base)]).astype(jnp.int32)

    def k_map(kb, info_ref):
        return (jnp.minimum(info_ref[3] + kb, info_ref[5]), 0)

    def v_map(kb, info_ref):
        return (jnp.minimum(info_ref[3] + kb, info_ref[5]), 1)

    grid_spec = pltpu.PrefetchScalarGridSpec(
        num_scalar_prefetch=1,
        grid=(steps,),
        in_specs=[
            pl.BlockSpec((rows, width), lambda kb, info_ref: (0, 0)),
            pl.BlockSpec((tk, width), k_map),
            pl.BlockSpec((tk, width), v_map),
        ],
        out_specs=[
            pl.BlockSpec((rows, width), lambda kb, info_ref: (0, 0)),
            pl.BlockSpec((heads, rows, HSIZE), lambda kb, info_ref: (0, 0, 0)),
        ],
        scratch_shapes=[
            pltpu.VMEM((heads, rows, HSIZE), jnp.float32),
            pltpu.VMEM((heads, rows, HSIZE), jnp.float32),
            pltpu.VMEM((heads, rows, HSIZE), jnp.float32),
        ],
    )
    keys = steps * tk
    return pl.pallas_call(
        self_kernel,
        grid_spec=grid_spec,
        out_shape=[
            jax.ShapeDtypeStruct((rows, width), jnp.float32),
            jax.ShapeDtypeStruct((heads, rows, HSIZE), jnp.float32),
        ],
        compiler_params=pltpu.CompilerParams(dimension_semantics=("arbitrary",)),
        cost_estimate=pl.CostEstimate(
            flops=2 * rows * keys * width,
            transcendentals=rows * keys * heads,
            bytes_accessed=keys * width * 4 + query.size * 2 + rows * width * 8,
        ),
    )(info, query, kv, kv)


def spread(lse):
    heads, rows, _ = lse.shape
    return jnp.broadcast_to(jnp.transpose(lse, (1, 0, 2)), (rows, heads, HSIZE)).reshape(
        rows, heads * HSIZE
    )


def cross_kernel(info_ref, q_ref, k_ref, v_ref, o_ref, m_ref, l_ref, acc_ref):
    kb = pl.program_id(1)
    nkb = pl.num_programs(1)
    tk = k_ref.shape[0]
    rows = q_ref.shape[0]
    last = info_ref[3]

    @pl.when(kb == 0)
    def _():
        m_ref[...] = jnp.full(m_ref.shape, NEG_FILL, jnp.float32)
        l_ref[...] = jnp.zeros(l_ref.shape, jnp.float32)
        acc_ref[...] = jnp.zeros(acc_ref.shape, jnp.float32)

    @pl.when(kb <= last)
    def _():
        r = lax.broadcasted_iota(jnp.int32, (rows, tk), 0)
        j = lax.broadcasted_iota(jnp.int32, (rows, tk), 1) + kb * tk
        span = r // SPAN
        limit = jnp.where(span == 0, info_ref[0], jnp.where(span == 1, info_ref[1], info_ref[2]))
        online_step(q_ref[...], k_ref[...], v_ref[...], j < limit * TBLK, m_ref, l_ref, acc_ref)

    @pl.when(kb == nkb - 1)
    def _():
        o_ref[...] = (acc_ref[...] / l_ref[...]).astype(o_ref.dtype)


def cross_attention(info, query, keys, values):
    rows = query.shape[0]
    heads = query.shape[1] // HSIZE
    tk = 512
    nkb = keys.shape[0] // tk

    def kv_map(h, kb, info_ref):
        return (jnp.minimum(kb, info_ref[3]), h)

    grid_spec = pltpu.PrefetchScalarGridSpec(
        num_scalar_prefetch=1,
        grid=(heads, nkb),
        in_specs=[
            pl.BlockSpec((rows, HSIZE), lambda h, kb, info_ref: (0, h)),
            pl.BlockSpec((tk, HSIZE), kv_map),
            pl.BlockSpec((tk, HSIZE), kv_map),
        ],
        out_specs=pl.BlockSpec((rows, HSIZE), lambda h, kb, info_ref: (0, h)),
        scratch_shapes=[
            pltpu.VMEM((rows, HSIZE), jnp.float32),
            pltpu.VMEM((rows, HSIZE), jnp.float32),
            pltpu.VMEM((rows, HSIZE), jnp.float32),
        ],
    )
    return pl.pallas_call(
        cross_kernel,
        grid_spec=grid_spec,
        out_shape=jax.ShapeDtypeStruct(query.shape, jnp.bfloat16),
        compiler_params=pltpu.CompilerParams(dimension_semantics=("arbitrary", "arbitrary")),
        cost_estimate=pl.CostEstimate(
            flops=4 * rows * keys.shape[0] * query.shape[1],
            transcendentals=rows * keys.shape[0] * heads,
            bytes_accessed=keys.size * 2 + values.size * 2 + query.size * 4,
        ),
    )(info, query, keys, values)


def per_device(self_q, self_k, self_v, cross_q, text_k, text_v, lags):
    rows = self_q.shape[0]
    tk = 2 * rows
    place = lax.axis_index("seq")

    whole_keys = lax.all_to_all(text_k, "txt", split_axis=1, concat_axis=0, tiled=True)
    whole_values = lax.all_to_all(text_v, "txt", split_axis=1, concat_axis=0, tiled=True)

    kv = lax.all_gather(jnp.concatenate([self_k, self_v], axis=1), "seq", axis=0, tiled=True)
    blocks = kv.shape[0] // rows
    half = blocks // 2
    pairs = [(i, blocks - 1 - i) for i in range(blocks)]
    partner = blocks - 1 - place
    heavy = place >= half
    other_q = lax.ppermute(self_q, "seq", pairs)

    b_hi = jnp.where(heavy, 0, half - 1 - place)
    o_b, lse_b = self_partial(partner, 0, b_hi, other_q, kv, tk, half // 2)
    a_lo = jnp.where(heavy, place - half, 0)
    o_a, lse_a = self_partial(place, a_lo, place + 1, self_q, kv, tk, (half + 1) // 2 + 1)
    o_a, lse_a, o_b, lse_b = lax.optimization_barrier((o_a, lse_a, o_b, lse_b))
    o_back = lax.ppermute(o_b, "seq", pairs)
    lse_back = lax.ppermute(lse_b[:, :, :1], "seq", pairs)
    la = spread(lse_a[:, :, :1])
    lb = spread(lse_back)
    peak = jnp.maximum(la, lb)
    w_a = jnp.exp2(la - peak)
    w_b = jnp.exp2(lb - peak)
    self_out = ((o_a * w_a + o_back * w_b) / (w_a + w_b)).astype(jnp.bfloat16)

    top = jnp.max(lags)
    cross_info = jnp.concatenate(
        [lags.astype(jnp.int32), ((top * TBLK - 1) // 512)[None].astype(jnp.int32)]
    )
    cross_out = cross_attention(cross_info, cross_q, whole_keys, whole_values)
    return (self_out, cross_out)


def solution(mesh):
    rows = P("seq", "txt")
    return jax.shard_map(
        per_device,
        mesh=mesh,
        in_specs=(rows, rows, rows, rows, P("txt", None), P("txt", None), P("seq")),
        out_specs=(rows, rows),
        check_vma=False,
    )
```

```python
import functools
import math

import jax
import jax.numpy as jnp
import numpy as np
from jax import lax
from jax.experimental import pallas as pl
from jax.experimental.pallas import tpu as pltpu
from jax.sharding import Mesh
from jax.sharding import PartitionSpec as P

HSIZE = 128
SPAN = 128
TBLK = 128

NEG_FILL = -1e30
FACTOR = 1.0 / math.sqrt(HSIZE)
SCALE2 = FACTOR * 1.4426950408889634


def online_step(q, k, v, mask, m_ref, l_ref, acc_ref):
    scores = (
        lax.dot_general(q, k, (((1,), (1,)), ((), ())), preferred_element_type=jnp.float32)
        * SCALE2
    )
    if mask is not None:
        scores = jnp.where(mask, scores, NEG_FILL)
    m_prev = m_ref[...]
    m_next = jnp.maximum(m_prev, jnp.max(scores, axis=1, keepdims=True))
    probs = jnp.exp2(scores - m_next[:, 0:1])
    if mask is not None:
        probs = jnp.where(mask, probs, 0.0)
    alpha = jnp.exp2(m_prev - m_next)
    extended = jnp.concatenate([v, jnp.ones_like(v)], axis=1)
    mixed = jnp.dot(probs.astype(jnp.bfloat16), extended, preferred_element_type=jnp.float32)
    l_ref[...] = alpha * l_ref[...] + mixed[:, HSIZE:]
    acc_ref[...] = acc_ref[...] * alpha + mixed[:, :HSIZE]
    m_ref[...] = m_next


def self_kernel(info_ref, q_ref, k_ref, v_ref, o_ref, lse_ref, m_ref, l_ref, acc_ref):
    kb = pl.program_id(0)
    nkb = pl.num_programs(0)
    qblk = info_ref[0]
    lo = info_ref[1]
    hi = info_ref[2]
    base = info_ref[3]
    top = info_ref[4]
    rows = q_ref.shape[0]
    tk = k_ref.shape[0]
    heads = q_ref.shape[1] // HSIZE
    blk = base + kb

    @pl.when(kb == 0)
    def _():
        m_ref[...] = jnp.full(m_ref.shape, NEG_FILL, jnp.float32)
        l_ref[...] = jnp.zeros(l_ref.shape, jnp.float32)
        acc_ref[...] = jnp.zeros(acc_ref.shape, jnp.float32)

    def run(mask):
        for h in range(heads):
            cols = slice(h * HSIZE, (h + 1) * HSIZE)
            online_step(
                q_ref[:, cols], k_ref[:, cols], v_ref[:, cols], mask,
                m_ref.at[h], l_ref.at[h], acc_ref.at[h],
            )

    live = blk <= top
    edge = jnp.logical_or(blk == base, blk == top)

    @pl.when(jnp.logical_and(live, jnp.logical_not(edge)))
    def _():
        run(None)

    @pl.when(jnp.logical_and(live, edge))
    def _():
        r = lax.broadcasted_iota(jnp.int32, (rows, tk), 0) + qblk * rows
        j = lax.broadcasted_iota(jnp.int32, (rows, tk), 1) + blk * tk
        inside = jnp.logical_and(j >= lo * rows, j < hi * rows)
        run(jnp.logical_and(j <= r, inside))

    @pl.when(kb == nkb - 1)
    def _():
        for h in range(heads):
            l = l_ref[h]
            seen = l > 0.0
            safe = jnp.where(seen, l, 1.0)
            o_ref[:, h * HSIZE:(h + 1) * HSIZE] = acc_ref[h] / safe
            lse_ref[h] = jnp.where(seen, m_ref[h] + jnp.log2(safe), NEG_FILL)


def self_partial(qblk, lo, hi, query, kv, tk, steps):
    rows, width = query.shape
    heads = width // HSIZE
    per = tk // rows
    base = lo // per
    top = jnp.where(hi > lo, (hi - 1) // per, base - 1)
    info = jnp.stack([qblk, lo, hi, base, top, jnp.maximum(top, base)]).astype(jnp.int32)

    def k_map(kb, info_ref):
        return (jnp.minimum(info_ref[3] + kb, info_ref[5]), 0)

    def v_map(kb, info_ref):
        return (jnp.minimum(info_ref[3] + kb, info_ref[5]), 1)

    grid_spec = pltpu.PrefetchScalarGridSpec(
        num_scalar_prefetch=1,
        grid=(steps,),
        in_specs=[
            pl.BlockSpec((rows, width), lambda kb, info_ref: (0, 0)),
            pl.BlockSpec((tk, width), k_map),
            pl.BlockSpec((tk, width), v_map),
        ],
        out_specs=[
            pl.BlockSpec((rows, width), lambda kb, info_ref: (0, 0)),
            pl.BlockSpec((heads, rows, HSIZE), lambda kb, info_ref: (0, 0, 0)),
        ],
        scratch_shapes=[
            pltpu.VMEM((heads, rows, HSIZE), jnp.float32),
            pltpu.VMEM((heads, rows, HSIZE), jnp.float32),
            pltpu.VMEM((heads, rows, HSIZE), jnp.float32),
        ],
    )
    keys = steps * tk
    return pl.pallas_call(
        self_kernel,
        grid_spec=grid_spec,
        out_shape=[
            jax.ShapeDtypeStruct((rows, width), jnp.float32),
            jax.ShapeDtypeStruct((heads, rows, HSIZE), jnp.float32),
        ],
        compiler_params=pltpu.CompilerParams(dimension_semantics=("arbitrary",)),
        cost_estimate=pl.CostEstimate(
            flops=2 * rows * keys * width,
            transcendentals=rows * keys * heads,
            bytes_accessed=keys * width * 4 + query.size * 2 + rows * width * 8,
        ),
    )(info, query, kv, kv)


def spread(lse):
    heads, rows, _ = lse.shape
    return jnp.broadcast_to(jnp.transpose(lse, (1, 0, 2)), (rows, heads, HSIZE)).reshape(
        rows, heads * HSIZE
    )


def cross_kernel(info_ref, q_ref, k_ref, v_ref, o_ref, m_ref, l_ref, acc_ref):
    kb = pl.program_id(1)
    nkb = pl.num_programs(1)
    tk = k_ref.shape[0]
    rows = q_ref.shape[0]
    last = info_ref[3]

    @pl.when(kb == 0)
    def _():
        m_ref[...] = jnp.full(m_ref.shape, NEG_FILL, jnp.float32)
        l_ref[...] = jnp.zeros(l_ref.shape, jnp.float32)
        acc_ref[...] = jnp.zeros(acc_ref.shape, jnp.float32)

    @pl.when(kb <= last)
    def _():
        r = lax.broadcasted_iota(jnp.int32, (rows, tk), 0)
        j = lax.broadcasted_iota(jnp.int32, (rows, tk), 1) + kb * tk
        span = r // SPAN
        limit = jnp.where(span == 0, info_ref[0], jnp.where(span == 1, info_ref[1], info_ref[2]))
        online_step(q_ref[...], k_ref[...], v_ref[...], j < limit * TBLK, m_ref, l_ref, acc_ref)

    @pl.when(kb == nkb - 1)
    def _():
        o_ref[...] = (acc_ref[...] / l_ref[...]).astype(o_ref.dtype)


def cross_attention(info, query, keys, values):
    rows = query.shape[0]
    heads = query.shape[1] // HSIZE
    tk = 512
    nkb = keys.shape[0] // tk

    def kv_map(h, kb, info_ref):
        return (jnp.minimum(kb, info_ref[3]), h)

    grid_spec = pltpu.PrefetchScalarGridSpec(
        num_scalar_prefetch=1,
        grid=(heads, nkb),
        in_specs=[
            pl.BlockSpec((rows, HSIZE), lambda h, kb, info_ref: (0, h)),
            pl.BlockSpec((tk, HSIZE), kv_map),
            pl.BlockSpec((tk, HSIZE), kv_map),
        ],
        out_specs=pl.BlockSpec((rows, HSIZE), lambda h, kb, info_ref: (0, h)),
        scratch_shapes=[
            pltpu.VMEM((rows, HSIZE), jnp.float32),
            pltpu.VMEM((rows, HSIZE), jnp.float32),
            pltpu.VMEM((rows, HSIZE), jnp.float32),
        ],
    )
    return pl.pallas_call(
        cross_kernel,
        grid_spec=grid_spec,
        out_shape=jax.ShapeDtypeStruct(query.shape, jnp.bfloat16),
        compiler_params=pltpu.CompilerParams(dimension_semantics=("arbitrary", "arbitrary")),
        cost_estimate=pl.CostEstimate(
            flops=4 * rows * keys.shape[0] * query.shape[1],
            transcendentals=rows * keys.shape[0] * heads,
            bytes_accessed=keys.size * 2 + values.size * 2 + query.size * 4,
        ),
    )(info, query, keys, values)


def per_device(self_q, self_k, self_v, cross_q, text_k, text_v, lags):
    rows = self_q.shape[0]
    tk = 2 * rows
    place = lax.axis_index("seq")

    whole_keys = lax.all_to_all(text_k, "txt", split_axis=1, concat_axis=0, tiled=True)
    whole_values = lax.all_to_all(text_v, "txt", split_axis=1, concat_axis=0, tiled=True)

    top = jnp.max(lags)
    cross_info = jnp.concatenate(
        [lags.astype(jnp.int32), ((top * TBLK - 1) // 512)[None].astype(jnp.int32)]
    )
    cross_out = cross_attention(cross_info, cross_q, whole_keys, whole_values)

    kv = lax.all_gather(jnp.concatenate([self_k, self_v], axis=1), "seq", axis=0, tiled=True)
    kv, cross_out = lax.optimization_barrier((kv, cross_out))
    blocks = kv.shape[0] // rows
    half = blocks // 2
    pairs = [(i, blocks - 1 - i) for i in range(blocks)]
    partner = blocks - 1 - place
    heavy = place >= half
    other_q = lax.ppermute(self_q, "seq", pairs)

    b_hi = jnp.where(heavy, 0, half - 1 - place)
    o_b, lse_b = self_partial(partner, 0, b_hi, other_q, kv, tk, half // 2)
    a_lo = jnp.where(heavy, place - half, 0)
    o_a, lse_a = self_partial(place, a_lo, place + 1, self_q, kv, tk, (half + 1) // 2 + 1)
    o_a, lse_a, o_b, lse_b = lax.optimization_barrier((o_a, lse_a, o_b, lse_b))
    o_back = lax.ppermute(o_b, "seq", pairs)
    lse_back = lax.ppermute(lse_b[:, :, :1], "seq", pairs)
    la = spread(lse_a[:, :, :1])
    lb = spread(lse_back)
    peak = jnp.maximum(la, lb)
    w_a = jnp.exp2(la - peak)
    w_b = jnp.exp2(lb - peak)
    self_out = ((o_a * w_a + o_back * w_b) / (w_a + w_b)).astype(jnp.bfloat16)

    return (self_out, cross_out)


def solution(mesh):
    rows = P("seq", "txt")
    return jax.shard_map(
        per_device,
        mesh=mesh,
        in_specs=(rows, rows, rows, rows, P("txt", None), P("txt", None), P("seq")),
        out_specs=(rows, rows),
        check_vma=False,
    )
```

```python
import functools
import math

import jax
import jax.numpy as jnp
import numpy as np
from jax import lax
from jax.experimental import pallas as pl
from jax.experimental.pallas import tpu as pltpu
from jax.sharding import Mesh
from jax.sharding import PartitionSpec as P

HSIZE = 128
SPAN = 128
TBLK = 128

NEG_FILL = -1e30
FACTOR = 1.0 / math.sqrt(HSIZE)
SCALE2 = FACTOR * 1.4426950408889634


def online_step(q, k, v, mask, m_ref, l_ref, acc_ref):
    scores = (
        lax.dot_general(q, k, (((1,), (1,)), ((), ())), preferred_element_type=jnp.float32)
        * SCALE2
    )
    if mask is not None:
        scores = jnp.where(mask, scores, NEG_FILL)
    m_prev = m_ref[...]
    m_next = jnp.maximum(m_prev, jnp.max(scores, axis=1, keepdims=True))
    probs = jnp.exp2(scores - m_next[:, 0:1])
    if mask is not None:
        probs = jnp.where(mask, probs, 0.0)
    alpha = jnp.exp2(m_prev - m_next)
    extended = jnp.concatenate([v, jnp.ones_like(v)], axis=1)
    mixed = jnp.dot(probs.astype(jnp.bfloat16), extended, preferred_element_type=jnp.float32)
    l_ref[...] = alpha * l_ref[...] + mixed[:, HSIZE:]
    acc_ref[...] = acc_ref[...] * alpha + mixed[:, :HSIZE]
    m_ref[...] = m_next


def self_kernel(info_ref, q_ref, k_ref, v_ref, o_ref, lse_ref, m_ref, l_ref, acc_ref):
    kb = pl.program_id(0)
    nkb = pl.num_programs(0)
    qblk = info_ref[0]
    lo = info_ref[1]
    hi = info_ref[2]
    base = info_ref[3]
    top = info_ref[4]
    rows = q_ref.shape[0]
    tk = k_ref.shape[0]
    heads = q_ref.shape[1] // HSIZE
    blk = base + kb

    @pl.when(kb == 0)
    def _():
        m_ref[...] = jnp.full(m_ref.shape, NEG_FILL, jnp.float32)
        l_ref[...] = jnp.zeros(l_ref.shape, jnp.float32)
        acc_ref[...] = jnp.zeros(acc_ref.shape, jnp.float32)

    def run(mask):
        for h in range(heads):
            cols = slice(h * HSIZE, (h + 1) * HSIZE)
            online_step(
                q_ref[:, cols], k_ref[:, cols], v_ref[:, cols], mask,
                m_ref.at[h], l_ref.at[h], acc_ref.at[h],
            )

    live = blk <= top
    edge = jnp.logical_or(blk == base, blk == top)

    @pl.when(jnp.logical_and(live, jnp.logical_not(edge)))
    def _():
        run(None)

    @pl.when(jnp.logical_and(live, edge))
    def _():
        r = lax.broadcasted_iota(jnp.int32, (rows, tk), 0) + qblk * rows
        j = lax.broadcasted_iota(jnp.int32, (rows, tk), 1) + blk * tk
        inside = jnp.logical_and(j >= lo * rows, j < hi * rows)
        run(jnp.logical_and(j <= r, inside))

    @pl.when(kb == nkb - 1)
    def _():
        for h in range(heads):
            l = l_ref[h]
            seen = l > 0.0
            safe = jnp.where(seen, l, 1.0)
            o_ref[:, h * HSIZE:(h + 1) * HSIZE] = acc_ref[h] / safe
            lse_ref[h] = jnp.where(seen, m_ref[h] + jnp.log2(safe), NEG_FILL)


def self_partial(qblk, lo, hi, query, kv, tk, steps):
    rows, width = query.shape
    heads = width // HSIZE
    per = tk // rows
    base = lo // per
    top = jnp.where(hi > lo, (hi - 1) // per, base - 1)
    info = jnp.stack([qblk, lo, hi, base, top, jnp.maximum(top, base)]).astype(jnp.int32)

    def k_map(kb, info_ref):
        return (jnp.minimum(info_ref[3] + kb, info_ref[5]), 0)

    def v_map(kb, info_ref):
        return (jnp.minimum(info_ref[3] + kb, info_ref[5]), 1)

    grid_spec = pltpu.PrefetchScalarGridSpec(
        num_scalar_prefetch=1,
        grid=(steps,),
        in_specs=[
            pl.BlockSpec((rows, width), lambda kb, info_ref: (0, 0)),
            pl.BlockSpec((tk, width), k_map),
            pl.BlockSpec((tk, width), v_map),
        ],
        out_specs=[
            pl.BlockSpec((rows, width), lambda kb, info_ref: (0, 0)),
            pl.BlockSpec((heads, rows, HSIZE), lambda kb, info_ref: (0, 0, 0)),
        ],
        scratch_shapes=[
            pltpu.VMEM((heads, rows, HSIZE), jnp.float32),
            pltpu.VMEM((heads, rows, HSIZE), jnp.float32),
            pltpu.VMEM((heads, rows, HSIZE), jnp.float32),
        ],
    )
    keys = steps * tk
    return pl.pallas_call(
        self_kernel,
        grid_spec=grid_spec,
        out_shape=[
            jax.ShapeDtypeStruct((rows, width), jnp.float32),
            jax.ShapeDtypeStruct((heads, rows, HSIZE), jnp.float32),
        ],
        compiler_params=pltpu.CompilerParams(dimension_semantics=("arbitrary",)),
        cost_estimate=pl.CostEstimate(
            flops=2 * rows * keys * width,
            transcendentals=rows * keys * heads,
            bytes_accessed=keys * width * 4 + query.size * 2 + rows * width * 8,
        ),
    )(info, query, kv, kv)


def spread(lse):
    heads, rows, _ = lse.shape
    return jnp.broadcast_to(jnp.transpose(lse, (1, 0, 2)), (rows, heads, HSIZE)).reshape(
        rows, heads * HSIZE
    )


def cross_kernel(info_ref, q_ref, k_ref, v_ref, o_ref, m_ref, l_ref, acc_ref):
    kb = pl.program_id(1)
    nkb = pl.num_programs(1)
    tk = k_ref.shape[0]
    rows = q_ref.shape[0]
    last = info_ref[3]

    @pl.when(kb == 0)
    def _():
        m_ref[...] = jnp.full(m_ref.shape, NEG_FILL, jnp.float32)
        l_ref[...] = jnp.zeros(l_ref.shape, jnp.float32)
        acc_ref[...] = jnp.zeros(acc_ref.shape, jnp.float32)

    @pl.when(kb <= last)
    def _():
        r = lax.broadcasted_iota(jnp.int32, (rows, tk), 0)
        j = lax.broadcasted_iota(jnp.int32, (rows, tk), 1) + kb * tk
        span = r // SPAN
        limit = jnp.where(span == 0, info_ref[0], jnp.where(span == 1, info_ref[1], info_ref[2]))
        online_step(q_ref[...], k_ref[...], v_ref[...], j < limit * TBLK, m_ref, l_ref, acc_ref)

    @pl.when(kb == nkb - 1)
    def _():
        o_ref[...] = (acc_ref[...] / l_ref[...]).astype(o_ref.dtype)


def cross_attention(info, query, keys, values):
    rows = query.shape[0]
    heads = query.shape[1] // HSIZE
    tk = 512
    nkb = keys.shape[0] // tk

    def kv_map(h, kb, info_ref):
        return (jnp.minimum(kb, info_ref[3]), h)

    grid_spec = pltpu.PrefetchScalarGridSpec(
        num_scalar_prefetch=1,
        grid=(heads, nkb),
        in_specs=[
            pl.BlockSpec((rows, HSIZE), lambda h, kb, info_ref: (0, h)),
            pl.BlockSpec((tk, HSIZE), kv_map),
            pl.BlockSpec((tk, HSIZE), kv_map),
        ],
        out_specs=pl.BlockSpec((rows, HSIZE), lambda h, kb, info_ref: (0, h)),
        scratch_shapes=[
            pltpu.VMEM((rows, HSIZE), jnp.float32),
            pltpu.VMEM((rows, HSIZE), jnp.float32),
            pltpu.VMEM((rows, HSIZE), jnp.float32),
        ],
    )
    return pl.pallas_call(
        cross_kernel,
        grid_spec=grid_spec,
        out_shape=jax.ShapeDtypeStruct(query.shape, jnp.bfloat16),
        compiler_params=pltpu.CompilerParams(dimension_semantics=("arbitrary", "arbitrary")),
        cost_estimate=pl.CostEstimate(
            flops=4 * rows * keys.shape[0] * query.shape[1],
            transcendentals=rows * keys.shape[0] * heads,
            bytes_accessed=keys.size * 2 + values.size * 2 + query.size * 4,
        ),
    )(info, query, keys, values)


def per_device(self_q, self_k, self_v, cross_q, text_k, text_v, lags):
    rows = self_q.shape[0]
    tk = 2 * rows
    place = lax.axis_index("seq")

    whole_keys = lax.all_to_all(text_k, "txt", split_axis=1, concat_axis=0, tiled=True)
    whole_values = lax.all_to_all(text_v, "txt", split_axis=1, concat_axis=0, tiled=True)

    top = jnp.max(lags)
    cross_info = jnp.concatenate(
        [lags.astype(jnp.int32), ((top * TBLK - 1) // 512)[None].astype(jnp.int32)]
    )
    cross_out = cross_attention(cross_info, cross_q, whole_keys, whole_values)

    kv = lax.all_gather(jnp.concatenate([self_k, self_v], axis=1), "seq", axis=0, tiled=True)
    kv, cross_out = lax.optimization_barrier((kv, cross_out))
    blocks = kv.shape[0] // rows
    half = blocks // 2
    pairs = [(i, blocks - 1 - i) for i in range(blocks)]
    partner = blocks - 1 - place
    heavy = place >= half
    other_q = lax.ppermute(self_q, "seq", pairs)

    b_hi = jnp.where(heavy, 0, half - 1 - place)
    o_b, lse_b = self_partial(partner, 0, b_hi, other_q, kv, tk, half // 2)
    a_lo = jnp.where(heavy, place - half, 0)
    o_a, lse_a = self_partial(place, a_lo, place + 1, self_q, kv, tk, (half + 1) // 2 + 1)
    o_a, lse_a, o_b, lse_b = lax.optimization_barrier((o_a, lse_a, o_b, lse_b))
    heads = lse_b.shape[0]
    width = o_b.shape[1]
    packed = jnp.concatenate([o_b, lse_b[:, :, 0].reshape(heads * rows // width, width)], axis=0)
    packed = lax.ppermute(packed, "seq", pairs)
    o_back = packed[:rows]
    lse_back = packed[rows:].reshape(heads, rows, 1)
    la = spread(lse_a[:, :, :1])
    lb = spread(lse_back)
    peak = jnp.maximum(la, lb)
    w_a = jnp.exp2(la - peak)
    w_b = jnp.exp2(lb - peak)
    self_out = ((o_a * w_a + o_back * w_b) / (w_a + w_b)).astype(jnp.bfloat16)

    return (self_out, cross_out)


def solution(mesh):
    rows = P("seq", "txt")
    return jax.shard_map(
        per_device,
        mesh=mesh,
        in_specs=(rows, rows, rows, rows, P("txt", None), P("txt", None), P("seq")),
        out_specs=(rows, rows),
        check_vma=False,
    )
```

```python
import functools
import math

import jax
import jax.numpy as jnp
import numpy as np
from jax import lax
from jax.experimental import pallas as pl
from jax.experimental.pallas import tpu as pltpu
from jax.sharding import Mesh
from jax.sharding import PartitionSpec as P

HSIZE = 128
SPAN = 128
TBLK = 128

NEG_FILL = -1e30
FACTOR = 1.0 / math.sqrt(HSIZE)
SCALE2 = FACTOR * 1.4426950408889634


def online_step(q, k, v, mask, m_ref, l_ref, acc_ref):
    scores = (
        lax.dot_general(q, k, (((1,), (1,)), ((), ())), preferred_element_type=jnp.float32)
        * SCALE2
    )
    if mask is not None:
        scores = jnp.where(mask, scores, NEG_FILL)
    m_prev = m_ref[...]
    m_next = jnp.maximum(m_prev, jnp.max(scores, axis=1, keepdims=True))
    probs = jnp.exp2(scores - m_next[:, 0:1])
    if mask is not None:
        probs = jnp.where(mask, probs, 0.0)
    alpha = jnp.exp2(m_prev - m_next)
    extended = jnp.concatenate([v, jnp.ones_like(v)], axis=1)
    mixed = jnp.dot(probs.astype(jnp.bfloat16), extended, preferred_element_type=jnp.float32)
    l_ref[...] = alpha * l_ref[...] + mixed[:, HSIZE:]
    acc_ref[...] = acc_ref[...] * alpha + mixed[:, :HSIZE]
    m_ref[...] = m_next


def self_kernel(info_ref, q_ref, k_ref, v_ref, o_ref, m_ref, l_ref, acc_ref):
    kb = pl.program_id(0)
    nkb = pl.num_programs(0)
    place = info_ref[0]
    last = info_ref[1]
    rows = q_ref.shape[0]
    tk = k_ref.shape[0]
    heads = q_ref.shape[1] // HSIZE

    @pl.when(kb == 0)
    def _():
        m_ref[...] = jnp.full(m_ref.shape, NEG_FILL, jnp.float32)
        l_ref[...] = jnp.zeros(l_ref.shape, jnp.float32)
        acc_ref[...] = jnp.zeros(acc_ref.shape, jnp.float32)

    def run(mask):
        for h in range(heads):
            cols = slice(h * HSIZE, (h + 1) * HSIZE)
            online_step(
                q_ref[:, cols], k_ref[:, cols], v_ref[:, cols], mask,
                m_ref.at[h], l_ref.at[h], acc_ref.at[h],
            )

    @pl.when(kb < last)
    def _():
        run(None)

    @pl.when(kb == last)
    def _():
        r = lax.broadcasted_iota(jnp.int32, (rows, tk), 0) + place * rows
        j = lax.broadcasted_iota(jnp.int32, (rows, tk), 1) + kb * tk
        run(j <= r)

    @pl.when(kb == nkb - 1)
    def _():
        for h in range(heads):
            o_ref[:, h * HSIZE:(h + 1) * HSIZE] = (acc_ref[h] / l_ref[h]).astype(o_ref.dtype)


def self_attention(info, query, kv, tk):
    rows, width = query.shape
    heads = width // HSIZE
    nkb = kv.shape[0] // tk

    def k_map(kb, info_ref):
        return (jnp.minimum(kb, info_ref[1]), 0)

    def v_map(kb, info_ref):
        return (jnp.minimum(kb, info_ref[1]), 1)

    grid_spec = pltpu.PrefetchScalarGridSpec(
        num_scalar_prefetch=1,
        grid=(nkb,),
        in_specs=[
            pl.BlockSpec((rows, width), lambda kb, info_ref: (0, 0)),
            pl.BlockSpec((tk, width), k_map),
            pl.BlockSpec((tk, width), v_map),
        ],
        out_specs=pl.BlockSpec((rows, width), lambda kb, info_ref: (0, 0)),
        scratch_shapes=[
            pltpu.VMEM((heads, rows, HSIZE), jnp.float32),
            pltpu.VMEM((heads, rows, HSIZE), jnp.float32),
            pltpu.VMEM((heads, rows, HSIZE), jnp.float32),
        ],
    )
    keys = kv.shape[0]
    return pl.pallas_call(
        self_kernel,
        grid_spec=grid_spec,
        out_shape=jax.ShapeDtypeStruct(query.shape, jnp.bfloat16),
        compiler_params=pltpu.CompilerParams(dimension_semantics=("arbitrary",)),
        cost_estimate=pl.CostEstimate(
            flops=2 * rows * keys * width,
            transcendentals=rows * keys * heads // 2,
            bytes_accessed=kv.size + query.size * 4,
        ),
    )(info, query, kv, kv)


def cross_kernel(info_ref, q_ref, k_ref, v_ref, o_ref, m_ref, l_ref, acc_ref):
    kb = pl.program_id(1)
    nkb = pl.num_programs(1)
    tk = k_ref.shape[0]
    rows = q_ref.shape[0]
    last = info_ref[3]

    @pl.when(kb == 0)
    def _():
        m_ref[...] = jnp.full(m_ref.shape, NEG_FILL, jnp.float32)
        l_ref[...] = jnp.zeros(l_ref.shape, jnp.float32)
        acc_ref[...] = jnp.zeros(acc_ref.shape, jnp.float32)

    @pl.when(kb <= last)
    def _():
        r = lax.broadcasted_iota(jnp.int32, (rows, tk), 0)
        j = lax.broadcasted_iota(jnp.int32, (rows, tk), 1) + kb * tk
        span = r // SPAN
        limit = jnp.where(span == 0, info_ref[0], jnp.where(span == 1, info_ref[1], info_ref[2]))
        online_step(q_ref[...], k_ref[...], v_ref[...], j < limit * TBLK, m_ref, l_ref, acc_ref)

    @pl.when(kb == nkb - 1)
    def _():
        o_ref[...] = (acc_ref[...] / l_ref[...]).astype(o_ref.dtype)


def cross_attention(info, query, keys, values):
    rows = query.shape[0]
    heads = query.shape[1] // HSIZE
    tk = 512
    nkb = keys.shape[0] // tk

    def kv_map(h, kb, info_ref):
        return (jnp.minimum(kb, info_ref[3]), h)

    grid_spec = pltpu.PrefetchScalarGridSpec(
        num_scalar_prefetch=1,
        grid=(heads, nkb),
        in_specs=[
            pl.BlockSpec((rows, HSIZE), lambda h, kb, info_ref: (0, h)),
            pl.BlockSpec((tk, HSIZE), kv_map),
            pl.BlockSpec((tk, HSIZE), kv_map),
        ],
        out_specs=pl.BlockSpec((rows, HSIZE), lambda h, kb, info_ref: (0, h)),
        scratch_shapes=[
            pltpu.VMEM((rows, HSIZE), jnp.float32),
            pltpu.VMEM((rows, HSIZE), jnp.float32),
            pltpu.VMEM((rows, HSIZE), jnp.float32),
        ],
    )
    return pl.pallas_call(
        cross_kernel,
        grid_spec=grid_spec,
        out_shape=jax.ShapeDtypeStruct(query.shape, jnp.bfloat16),
        compiler_params=pltpu.CompilerParams(dimension_semantics=("arbitrary", "arbitrary")),
        cost_estimate=pl.CostEstimate(
            flops=4 * rows * keys.shape[0] * query.shape[1],
            transcendentals=rows * keys.shape[0] * heads,
            bytes_accessed=keys.size * 2 + values.size * 2 + query.size * 4,
        ),
    )(info, query, keys, values)


def per_device(self_q, self_k, self_v, cross_q, text_k, text_v, lags):
    rows = self_q.shape[0]
    place = lax.axis_index("seq")

    whole_keys = lax.all_to_all(text_k, "txt", split_axis=1, concat_axis=0, tiled=True)
    whole_values = lax.all_to_all(text_v, "txt", split_axis=1, concat_axis=0, tiled=True)

    top = jnp.max(lags)
    cross_info = jnp.concatenate(
        [lags.astype(jnp.int32), ((top * TBLK - 1) // 512)[None].astype(jnp.int32)]
    )
    cross_out = cross_attention(cross_info, cross_q, whole_keys, whole_values)

    kv = lax.all_gather(jnp.concatenate([self_k, self_v], axis=1), "seq", axis=0, tiled=True)
    kv, cross_out = lax.optimization_barrier((kv, cross_out))
    tk = 4 * rows if kv.shape[0] % (4 * rows) == 0 else rows
    info = jnp.stack([place, (place * rows + rows - 1) // tk]).astype(jnp.int32)
    self_out = self_attention(info, self_q, kv, tk)
    return (self_out, cross_out)


def solution(mesh):
    rows = P("seq", "txt")
    return jax.shard_map(
        per_device,
        mesh=mesh,
        in_specs=(rows, rows, rows, rows, P("txt", None), P("txt", None), P("seq")),
        out_specs=(rows, rows),
        check_vma=False,
    )
```

```python
import functools
import math

import jax
import jax.numpy as jnp
import numpy as np
from jax import lax
from jax.experimental import pallas as pl
from jax.experimental.pallas import tpu as pltpu
from jax.sharding import Mesh
from jax.sharding import PartitionSpec as P

HSIZE = 128
SPAN = 128
TBLK = 128

NEG_FILL = -1e30
FACTOR = 1.0 / math.sqrt(HSIZE)
SCALE2 = FACTOR * 1.4426950408889634


def online_step(q, k, v, mask, m_ref, l_ref, acc_ref):
    scores = (
        lax.dot_general(q, k, (((1,), (1,)), ((), ())), preferred_element_type=jnp.float32)
        * SCALE2
    )
    if mask is not None:
        scores = jnp.where(mask, scores, NEG_FILL)
    m_prev = m_ref[...]
    m_next = jnp.maximum(m_prev, jnp.max(scores, axis=1, keepdims=True))
    probs = jnp.exp2(scores - m_next[:, 0:1])
    if mask is not None:
        probs = jnp.where(mask, probs, 0.0)
    alpha = jnp.exp2(m_prev - m_next)
    extended = jnp.concatenate([v, jnp.ones_like(v)], axis=1)
    mixed = jnp.dot(probs.astype(jnp.bfloat16), extended, preferred_element_type=jnp.float32)
    l_ref[...] = alpha * l_ref[...] + mixed[:, HSIZE:]
    acc_ref[...] = acc_ref[...] * alpha + mixed[:, :HSIZE]
    m_ref[...] = m_next


def self_kernel(info_ref, q_ref, k_ref, v_ref, o_ref, m_ref, l_ref, acc_ref):
    kb = pl.program_id(0)
    nkb = pl.num_programs(0)
    place = info_ref[0]
    last = info_ref[1]
    rows = q_ref.shape[0]
    tk = k_ref.shape[0]
    heads = q_ref.shape[1] // HSIZE

    @pl.when(kb == 0)
    def _():
        m_ref[...] = jnp.full(m_ref.shape, NEG_FILL, jnp.float32)
        l_ref[...] = jnp.zeros(l_ref.shape, jnp.float32)
        acc_ref[...] = jnp.zeros(acc_ref.shape, jnp.float32)

    def run(mask):
        for h in range(heads):
            cols = slice(h * HSIZE, (h + 1) * HSIZE)
            online_step(
                q_ref[:, cols], k_ref[:, cols], v_ref[:, cols], mask,
                m_ref.at[h], l_ref.at[h], acc_ref.at[h],
            )

    @pl.when(kb < last)
    def _():
        run(None)

    @pl.when(kb == last)
    def _():
        r = lax.broadcasted_iota(jnp.int32, (rows, tk), 0) + place * rows
        j = lax.broadcasted_iota(jnp.int32, (rows, tk), 1) + kb * tk
        run(j <= r)

    @pl.when(kb == nkb - 1)
    def _():
        for h in range(heads):
            o_ref[:, h * HSIZE:(h + 1) * HSIZE] = (acc_ref[h] / l_ref[h]).astype(o_ref.dtype)


def self_attention(info, query, kv, tk):
    rows, width = query.shape
    heads = width // HSIZE
    nkb = kv.shape[0] // tk

    def k_map(kb, info_ref):
        return (jnp.minimum(kb, info_ref[1]), 0)

    def v_map(kb, info_ref):
        return (jnp.minimum(kb, info_ref[1]), 1)

    grid_spec = pltpu.PrefetchScalarGridSpec(
        num_scalar_prefetch=1,
        grid=(nkb,),
        in_specs=[
            pl.BlockSpec((rows, width), lambda kb, info_ref: (0, 0)),
            pl.BlockSpec((tk, width), k_map),
            pl.BlockSpec((tk, width), v_map),
        ],
        out_specs=pl.BlockSpec((rows, width), lambda kb, info_ref: (0, 0)),
        scratch_shapes=[
            pltpu.VMEM((heads, rows, HSIZE), jnp.float32),
            pltpu.VMEM((heads, rows, HSIZE), jnp.float32),
            pltpu.VMEM((heads, rows, HSIZE), jnp.float32),
        ],
    )
    keys = kv.shape[0]
    return pl.pallas_call(
        self_kernel,
        grid_spec=grid_spec,
        out_shape=jax.ShapeDtypeStruct(query.shape, jnp.bfloat16),
        compiler_params=pltpu.CompilerParams(dimension_semantics=("arbitrary",)),
        cost_estimate=pl.CostEstimate(
            flops=2 * rows * keys * width,
            transcendentals=rows * keys * heads // 2,
            bytes_accessed=kv.size + query.size * 4,
        ),
    )(info, query, kv, kv)


def cross_kernel(info_ref, q_ref, k_ref, v_ref, o_ref, m_ref, l_ref, acc_ref):
    kb = pl.program_id(1)
    nkb = pl.num_programs(1)
    tk = k_ref.shape[0]
    rows = q_ref.shape[0]
    last = info_ref[3]

    @pl.when(kb == 0)
    def _():
        m_ref[...] = jnp.full(m_ref.shape, NEG_FILL, jnp.float32)
        l_ref[...] = jnp.zeros(l_ref.shape, jnp.float32)
        acc_ref[...] = jnp.zeros(acc_ref.shape, jnp.float32)

    @pl.when(kb <= last)
    def _():
        r = lax.broadcasted_iota(jnp.int32, (rows, tk), 0)
        j = lax.broadcasted_iota(jnp.int32, (rows, tk), 1) + kb * tk
        span = r // SPAN
        limit = jnp.where(span == 0, info_ref[0], jnp.where(span == 1, info_ref[1], info_ref[2]))
        online_step(q_ref[...], k_ref[...], v_ref[...], j < limit * TBLK, m_ref, l_ref, acc_ref)

    @pl.when(kb == nkb - 1)
    def _():
        o_ref[...] = (acc_ref[...] / l_ref[...]).astype(o_ref.dtype)


def cross_attention(info, query, keys, values):
    rows = query.shape[0]
    heads = query.shape[1] // HSIZE
    tk = 512
    nkb = keys.shape[0] // tk

    def kv_map(h, kb, info_ref):
        return (jnp.minimum(kb, info_ref[3]), h)

    grid_spec = pltpu.PrefetchScalarGridSpec(
        num_scalar_prefetch=1,
        grid=(heads, nkb),
        in_specs=[
            pl.BlockSpec((rows, HSIZE), lambda h, kb, info_ref: (0, h)),
            pl.BlockSpec((tk, HSIZE), kv_map),
            pl.BlockSpec((tk, HSIZE), kv_map),
        ],
        out_specs=pl.BlockSpec((rows, HSIZE), lambda h, kb, info_ref: (0, h)),
        scratch_shapes=[
            pltpu.VMEM((rows, HSIZE), jnp.float32),
            pltpu.VMEM((rows, HSIZE), jnp.float32),
            pltpu.VMEM((rows, HSIZE), jnp.float32),
        ],
    )
    return pl.pallas_call(
        cross_kernel,
        grid_spec=grid_spec,
        out_shape=jax.ShapeDtypeStruct(query.shape, jnp.bfloat16),
        compiler_params=pltpu.CompilerParams(dimension_semantics=("arbitrary", "arbitrary")),
        cost_estimate=pl.CostEstimate(
            flops=4 * rows * keys.shape[0] * query.shape[1],
            transcendentals=rows * keys.shape[0] * heads,
            bytes_accessed=keys.size * 2 + values.size * 2 + query.size * 4,
        ),
    )(info, query, keys, values)


def per_device(self_q, self_k, self_v, cross_q, text_k, text_v, lags):
    rows = self_q.shape[0]
    place = lax.axis_index("seq")

    whole_keys = lax.all_to_all(text_k, "txt", split_axis=1, concat_axis=0, tiled=True)
    whole_values = lax.all_to_all(text_v, "txt", split_axis=1, concat_axis=0, tiled=True)

    top = jnp.max(lags)
    cross_info = jnp.concatenate(
        [lags.astype(jnp.int32), ((top * TBLK - 1) // 512)[None].astype(jnp.int32)]
    )
    cross_out = cross_attention(cross_info, cross_q, whole_keys, whole_values)

    kv = lax.all_gather(jnp.concatenate([self_k, self_v], axis=1), "seq", axis=0, tiled=True)
    kv, cross_out = lax.optimization_barrier((kv, cross_out))
    tk = 8 * rows if kv.shape[0] % (8 * rows) == 0 else rows
    info = jnp.stack([place, (place * rows + rows - 1) // tk]).astype(jnp.int32)
    self_out = self_attention(info, self_q, kv, tk)
    return (self_out, cross_out)


def solution(mesh):
    rows = P("seq", "txt")
    return jax.shard_map(
        per_device,
        mesh=mesh,
        in_specs=(rows, rows, rows, rows, P("txt", None), P("txt", None), P("seq")),
        out_specs=(rows, rows),
        check_vma=False,
    )
```

```python
import functools
import math

import jax
import jax.numpy as jnp
import numpy as np
from jax import lax
from jax.experimental import pallas as pl
from jax.experimental.pallas import tpu as pltpu
from jax.sharding import Mesh
from jax.sharding import PartitionSpec as P

HSIZE = 128
SPAN = 128
TBLK = 128

NEG_FILL = -1e30
FACTOR = 1.0 / math.sqrt(HSIZE)
SCALE2 = FACTOR * 1.4426950408889634


def online_step(q, k, v, mask, m_ref, l_ref, acc_ref):
    scores = (
        lax.dot_general(q, k, (((1,), (1,)), ((), ())), preferred_element_type=jnp.float32)
        * SCALE2
    )
    if mask is not None:
        scores = jnp.where(mask, scores, NEG_FILL)
    m_prev = m_ref[...]
    m_next = jnp.maximum(m_prev, jnp.max(scores, axis=1, keepdims=True))
    probs = jnp.exp2(scores - m_next[:, 0:1])
    if mask is not None:
        probs = jnp.where(mask, probs, 0.0)
    alpha = jnp.exp2(m_prev - m_next)
    extended = jnp.concatenate([v, jnp.ones_like(v)], axis=1)
    mixed = jnp.dot(probs.astype(jnp.bfloat16), extended, preferred_element_type=jnp.float32)
    l_ref[...] = alpha * l_ref[...] + mixed[:, HSIZE:]
    acc_ref[...] = acc_ref[...] * alpha + mixed[:, :HSIZE]
    m_ref[...] = m_next


def self_kernel(info_ref, q_ref, k_ref, v_ref, o_ref, m_ref, l_ref, acc_ref):
    kb = pl.program_id(0)
    nkb = pl.num_programs(0)
    place = info_ref[0]
    last = info_ref[1]
    rows = q_ref.shape[0]
    tk = k_ref.shape[0]
    heads = q_ref.shape[1] // HSIZE

    @pl.when(kb == 0)
    def _():
        m_ref[...] = jnp.full(m_ref.shape, NEG_FILL, jnp.float32)
        l_ref[...] = jnp.zeros(l_ref.shape, jnp.float32)
        acc_ref[...] = jnp.zeros(acc_ref.shape, jnp.float32)

    def run(mask):
        for h in range(heads):
            cols = slice(h * HSIZE, (h + 1) * HSIZE)
            online_step(
                q_ref[:, cols], k_ref[:, cols], v_ref[:, cols], mask,
                m_ref.at[h], l_ref.at[h], acc_ref.at[h],
            )

    @pl.when(kb < last)
    def _():
        run(None)

    @pl.when(kb == last)
    def _():
        r = lax.broadcasted_iota(jnp.int32, (rows, tk), 0) + place * rows
        j = lax.broadcasted_iota(jnp.int32, (rows, tk), 1) + kb * tk
        run(j <= r)

    @pl.when(kb == nkb - 1)
    def _():
        for h in range(heads):
            o_ref[:, h * HSIZE:(h + 1) * HSIZE] = (acc_ref[h] / l_ref[h]).astype(o_ref.dtype)


def self_attention(info, query, kv, tk):
    rows, width = query.shape
    heads = width // HSIZE
    nkb = kv.shape[0] // tk

    def k_map(kb, info_ref):
        return (jnp.minimum(kb, info_ref[1]), 0)

    def v_map(kb, info_ref):
        return (jnp.minimum(kb, info_ref[1]), 1)

    grid_spec = pltpu.PrefetchScalarGridSpec(
        num_scalar_prefetch=1,
        grid=(nkb,),
        in_specs=[
            pl.BlockSpec((rows, width), lambda kb, info_ref: (0, 0)),
            pl.BlockSpec((tk, width), k_map),
            pl.BlockSpec((tk, width), v_map),
        ],
        out_specs=pl.BlockSpec((rows, width), lambda kb, info_ref: (0, 0)),
        scratch_shapes=[
            pltpu.VMEM((heads, rows, HSIZE), jnp.float32),
            pltpu.VMEM((heads, rows, HSIZE), jnp.float32),
            pltpu.VMEM((heads, rows, HSIZE), jnp.float32),
        ],
    )
    keys = kv.shape[0]
    return pl.pallas_call(
        self_kernel,
        grid_spec=grid_spec,
        out_shape=jax.ShapeDtypeStruct(query.shape, jnp.bfloat16),
        compiler_params=pltpu.CompilerParams(dimension_semantics=("arbitrary",)),
        cost_estimate=pl.CostEstimate(
            flops=2 * rows * keys * width,
            transcendentals=rows * keys * heads // 2,
            bytes_accessed=kv.size + query.size * 4,
        ),
    )(info, query, kv, kv)


def cross_kernel(info_ref, q_ref, k_ref, v_ref, o_ref, m_ref, l_ref, acc_ref):
    kb = pl.program_id(1)
    nkb = pl.num_programs(1)
    tk = k_ref.shape[0]
    rows = q_ref.shape[0]
    last = info_ref[3]

    @pl.when(kb == 0)
    def _():
        m_ref[...] = jnp.full(m_ref.shape, NEG_FILL, jnp.float32)
        l_ref[...] = jnp.zeros(l_ref.shape, jnp.float32)
        acc_ref[...] = jnp.zeros(acc_ref.shape, jnp.float32)

    @pl.when(kb <= last)
    def _():
        r = lax.broadcasted_iota(jnp.int32, (rows, tk), 0)
        j = lax.broadcasted_iota(jnp.int32, (rows, tk), 1) + kb * tk
        span = r // SPAN
        limit = jnp.where(span == 0, info_ref[0], jnp.where(span == 1, info_ref[1], info_ref[2]))
        online_step(q_ref[...], k_ref[...], v_ref[...], j < limit * TBLK, m_ref, l_ref, acc_ref)

    @pl.when(kb == nkb - 1)
    def _():
        o_ref[...] = (acc_ref[...] / l_ref[...]).astype(o_ref.dtype)


def cross_attention(info, query, keys, values):
    rows = query.shape[0]
    heads = query.shape[1] // HSIZE
    tk = 512
    nkb = keys.shape[0] // tk

    def kv_map(h, kb, info_ref):
        return (jnp.minimum(kb, info_ref[3]), h)

    grid_spec = pltpu.PrefetchScalarGridSpec(
        num_scalar_prefetch=1,
        grid=(heads, nkb),
        in_specs=[
            pl.BlockSpec((rows, HSIZE), lambda h, kb, info_ref: (0, h)),
            pl.BlockSpec((tk, HSIZE), kv_map),
            pl.BlockSpec((tk, HSIZE), kv_map),
        ],
        out_specs=pl.BlockSpec((rows, HSIZE), lambda h, kb, info_ref: (0, h)),
        scratch_shapes=[
            pltpu.VMEM((rows, HSIZE), jnp.float32),
            pltpu.VMEM((rows, HSIZE), jnp.float32),
            pltpu.VMEM((rows, HSIZE), jnp.float32),
        ],
    )
    return pl.pallas_call(
        cross_kernel,
        grid_spec=grid_spec,
        out_shape=jax.ShapeDtypeStruct(query.shape, jnp.bfloat16),
        compiler_params=pltpu.CompilerParams(dimension_semantics=("arbitrary", "arbitrary")),
        cost_estimate=pl.CostEstimate(
            flops=4 * rows * keys.shape[0] * query.shape[1],
            transcendentals=rows * keys.shape[0] * heads,
            bytes_accessed=keys.size * 2 + values.size * 2 + query.size * 4,
        ),
    )(info, query, keys, values)


def per_device(self_q, self_k, self_v, cross_q, text_k, text_v, lags):
    rows = self_q.shape[0]
    place = lax.axis_index("seq")

    whole_keys = lax.all_to_all(text_k, "txt", split_axis=1, concat_axis=0, tiled=True)
    whole_values = lax.all_to_all(text_v, "txt", split_axis=1, concat_axis=0, tiled=True)

    top = jnp.max(lags)
    cross_info = jnp.concatenate(
        [lags.astype(jnp.int32), ((top * TBLK - 1) // 512)[None].astype(jnp.int32)]
    )
    cross_out = cross_attention(cross_info, cross_q, whole_keys, whole_values)

    kv = lax.all_gather(jnp.concatenate([self_k, self_v], axis=1), "seq", axis=0, tiled=True)
    kv, cross_out = lax.optimization_barrier((kv, cross_out))
    tk = 16 * rows if kv.shape[0] % (16 * rows) == 0 else rows
    info = jnp.stack([place, (place * rows + rows - 1) // tk]).astype(jnp.int32)
    self_out = self_attention(info, self_q, kv, tk)
    return (self_out, cross_out)


def solution(mesh):
    rows = P("seq", "txt")
    return jax.shard_map(
        per_device,
        mesh=mesh,
        in_specs=(rows, rows, rows, rows, P("txt", None), P("txt", None), P("seq")),
        out_specs=(rows, rows),
        check_vma=False,
    )
```

```python
import functools
import math

import jax
import jax.numpy as jnp
import numpy as np
from jax import lax
from jax.experimental import pallas as pl
from jax.experimental.pallas import tpu as pltpu
from jax.sharding import Mesh
from jax.sharding import PartitionSpec as P

HSIZE = 128
SPAN = 128
TBLK = 128

NEG_FILL = -1e30
FACTOR = 1.0 / math.sqrt(HSIZE)
SCALE2 = FACTOR * 1.4426950408889634


def online_step(q, k, v, mask, m_ref, l_ref, acc_ref):
    scores = (
        lax.dot_general(q, k, (((1,), (1,)), ((), ())), preferred_element_type=jnp.float32)
        * SCALE2
    )
    if mask is not None:
        scores = jnp.where(mask, scores, NEG_FILL)
    m_prev = m_ref[...]
    m_next = jnp.maximum(m_prev, jnp.max(scores, axis=1, keepdims=True))
    probs = jnp.exp2(scores - m_next[:, 0:1])
    if mask is not None:
        probs = jnp.where(mask, probs, 0.0)
    alpha = jnp.exp2(m_prev - m_next)
    extended = jnp.concatenate([v, jnp.ones_like(v)], axis=1)
    mixed = jnp.dot(probs.astype(jnp.bfloat16), extended, preferred_element_type=jnp.float32)
    l_ref[...] = alpha * l_ref[...] + mixed[:, HSIZE:]
    acc_ref[...] = acc_ref[...] * alpha + mixed[:, :HSIZE]
    m_ref[...] = m_next


def self_kernel(info_ref, q_ref, k_ref, v_ref, o_ref, m_ref, l_ref, acc_ref):
    kb = pl.program_id(0)
    nkb = pl.num_programs(0)
    place = info_ref[0]
    last = info_ref[1]
    rows = q_ref.shape[0]
    tk = k_ref.shape[0]
    heads = q_ref.shape[1] // HSIZE

    @pl.when(kb == 0)
    def _():
        m_ref[...] = jnp.full(m_ref.shape, NEG_FILL, jnp.float32)
        l_ref[...] = jnp.zeros(l_ref.shape, jnp.float32)
        acc_ref[...] = jnp.zeros(acc_ref.shape, jnp.float32)

    def run(mask):
        for h in range(heads):
            cols = slice(h * HSIZE, (h + 1) * HSIZE)
            online_step(
                q_ref[:, cols], k_ref[:, cols], v_ref[:, cols], mask,
                m_ref.at[h], l_ref.at[h], acc_ref.at[h],
            )

    @pl.when(kb < last)
    def _():
        run(None)

    diag = place - kb * (tk // rows)
    for piece in range(tk // rows):
        keys = slice(piece * rows, (piece + 1) * rows)

        @pl.when(jnp.logical_and(kb == last, piece < diag))
        def _():
            for h in range(heads):
                cols = slice(h * HSIZE, (h + 1) * HSIZE)
                online_step(
                    q_ref[:, cols], k_ref[keys, cols], v_ref[keys, cols], None,
                    m_ref.at[h], l_ref.at[h], acc_ref.at[h],
                )

        @pl.when(jnp.logical_and(kb == last, piece == diag))
        def _():
            r = lax.broadcasted_iota(jnp.int32, (rows, rows), 0)
            j = lax.broadcasted_iota(jnp.int32, (rows, rows), 1)
            for h in range(heads):
                cols = slice(h * HSIZE, (h + 1) * HSIZE)
                online_step(
                    q_ref[:, cols], k_ref[keys, cols], v_ref[keys, cols], j <= r,
                    m_ref.at[h], l_ref.at[h], acc_ref.at[h],
                )

    @pl.when(kb == nkb - 1)
    def _():
        for h in range(heads):
            o_ref[:, h * HSIZE:(h + 1) * HSIZE] = (acc_ref[h] / l_ref[h]).astype(o_ref.dtype)


def self_attention(info, query, kv, tk):
    rows, width = query.shape
    heads = width // HSIZE
    nkb = kv.shape[0] // tk

    def k_map(kb, info_ref):
        return (jnp.minimum(kb, info_ref[1]), 0)

    def v_map(kb, info_ref):
        return (jnp.minimum(kb, info_ref[1]), 1)

    grid_spec = pltpu.PrefetchScalarGridSpec(
        num_scalar_prefetch=1,
        grid=(nkb,),
        in_specs=[
            pl.BlockSpec((rows, width), lambda kb, info_ref: (0, 0)),
            pl.BlockSpec((tk, width), k_map),
            pl.BlockSpec((tk, width), v_map),
        ],
        out_specs=pl.BlockSpec((rows, width), lambda kb, info_ref: (0, 0)),
        scratch_shapes=[
            pltpu.VMEM((heads, rows, HSIZE), jnp.float32),
            pltpu.VMEM((heads, rows, HSIZE), jnp.float32),
            pltpu.VMEM((heads, rows, HSIZE), jnp.float32),
        ],
    )
    keys = kv.shape[0]
    return pl.pallas_call(
        self_kernel,
        grid_spec=grid_spec,
        out_shape=jax.ShapeDtypeStruct(query.shape, jnp.bfloat16),
        compiler_params=pltpu.CompilerParams(dimension_semantics=("arbitrary",)),
        cost_estimate=pl.CostEstimate(
            flops=2 * rows * keys * width,
            transcendentals=rows * keys * heads // 2,
            bytes_accessed=kv.size + query.size * 4,
        ),
    )(info, query, kv, kv)


def cross_kernel(info_ref, q_ref, k_ref, v_ref, o_ref, m_ref, l_ref, acc_ref):
    kb = pl.program_id(1)
    nkb = pl.num_programs(1)
    tk = k_ref.shape[0]
    rows = q_ref.shape[0]
    last = info_ref[3]

    @pl.when(kb == 0)
    def _():
        m_ref[...] = jnp.full(m_ref.shape, NEG_FILL, jnp.float32)
        l_ref[...] = jnp.zeros(l_ref.shape, jnp.float32)
        acc_ref[...] = jnp.zeros(acc_ref.shape, jnp.float32)

    @pl.when(kb <= last)
    def _():
        r = lax.broadcasted_iota(jnp.int32, (rows, tk), 0)
        j = lax.broadcasted_iota(jnp.int32, (rows, tk), 1) + kb * tk
        span = r // SPAN
        limit = jnp.where(span == 0, info_ref[0], jnp.where(span == 1, info_ref[1], info_ref[2]))
        online_step(q_ref[...], k_ref[...], v_ref[...], j < limit * TBLK, m_ref, l_ref, acc_ref)

    @pl.when(kb == nkb - 1)
    def _():
        o_ref[...] = (acc_ref[...] / l_ref[...]).astype(o_ref.dtype)


def cross_attention(info, query, keys, values):
    rows = query.shape[0]
    heads = query.shape[1] // HSIZE
    tk = 512
    nkb = keys.shape[0] // tk

    def kv_map(h, kb, info_ref):
        return (jnp.minimum(kb, info_ref[3]), h)

    grid_spec = pltpu.PrefetchScalarGridSpec(
        num_scalar_prefetch=1,
        grid=(heads, nkb),
        in_specs=[
            pl.BlockSpec((rows, HSIZE), lambda h, kb, info_ref: (0, h)),
            pl.BlockSpec((tk, HSIZE), kv_map),
            pl.BlockSpec((tk, HSIZE), kv_map),
        ],
        out_specs=pl.BlockSpec((rows, HSIZE), lambda h, kb, info_ref: (0, h)),
        scratch_shapes=[
            pltpu.VMEM((rows, HSIZE), jnp.float32),
            pltpu.VMEM((rows, HSIZE), jnp.float32),
            pltpu.VMEM((rows, HSIZE), jnp.float32),
        ],
    )
    return pl.pallas_call(
        cross_kernel,
        grid_spec=grid_spec,
        out_shape=jax.ShapeDtypeStruct(query.shape, jnp.bfloat16),
        compiler_params=pltpu.CompilerParams(dimension_semantics=("arbitrary", "arbitrary")),
        cost_estimate=pl.CostEstimate(
            flops=4 * rows * keys.shape[0] * query.shape[1],
            transcendentals=rows * keys.shape[0] * heads,
            bytes_accessed=keys.size * 2 + values.size * 2 + query.size * 4,
        ),
    )(info, query, keys, values)


def per_device(self_q, self_k, self_v, cross_q, text_k, text_v, lags):
    rows = self_q.shape[0]
    place = lax.axis_index("seq")

    whole_keys = lax.all_to_all(text_k, "txt", split_axis=1, concat_axis=0, tiled=True)
    whole_values = lax.all_to_all(text_v, "txt", split_axis=1, concat_axis=0, tiled=True)

    top = jnp.max(lags)
    cross_info = jnp.concatenate(
        [lags.astype(jnp.int32), ((top * TBLK - 1) // 512)[None].astype(jnp.int32)]
    )
    cross_out = cross_attention(cross_info, cross_q, whole_keys, whole_values)

    kv = lax.all_gather(jnp.concatenate([self_k, self_v], axis=1), "seq", axis=0, tiled=True)
    kv, cross_out = lax.optimization_barrier((kv, cross_out))
    tk = 8 * rows if kv.shape[0] % (8 * rows) == 0 else rows
    info = jnp.stack([place, (place * rows + rows - 1) // tk]).astype(jnp.int32)
    self_out = self_attention(info, self_q, kv, tk)
    return (self_out, cross_out)


def solution(mesh):
    rows = P("seq", "txt")
    return jax.shard_map(
        per_device,
        mesh=mesh,
        in_specs=(rows, rows, rows, rows, P("txt", None), P("txt", None), P("seq")),
        out_specs=(rows, rows),
        check_vma=False,
    )
```
